32 devices in a mesh: dp: 4 (over x, core), mp: 8 (over z, y).
Axes of the slice: x: 2, y: 2, z: 4, core: 2. Of those that a mesh axis runs over, the one named last changes fastest.
Arguments:
- queries: bfloat16 [512, 4096], P('dp'), may hold values from -103 to 103
- new_kv: bfloat16 [2, 512, 1024], P(None, 'dp'), may hold values from -6 to 6
- residual: bfloat16 [512, 4096], P('dp', 'mp'), may hold values from -2.4 to 2.4
- out_weight: bfloat16 [4096, 4096], P('mp'), may hold values from -0.125 to 0.125
- norm_gain: float32 [4096], replicated, may hold values from 0.5 to 1.5
- router: bfloat16 [4096, 8], replicated, may hold values from -0.09375 to 0.09375
- expert_in: bfloat16 [8, 2, 8192, 4096], P('dp', None, 'mp'), may hold values from -0.09375 to 0.09375
- expert_out: bfloat16 [8, 8192, 4096], P('dp', 'mp'), may hold values from -0.09375 to 0.09375
- node_cache: bfloat16 [2, 384, 8, 128, 128], P(None, 'dp', 'mp'), may hold values from -6 to 6
- leaf_cache: bfloat16 [2, 512, 8, 128, 128], P(None, 'dp', 'mp'), may hold values from -6 to 6
- slot_request: int32 [512], replicated, may hold values from 0 to 511, each once
- request_branch: int32 [512], replicated, may hold values from 0 to 31, as said below
- branch_parent: int32 [32], replicated, may hold values from 0 to 7, as said below
- root_owner: int32 [8], replicated, may hold values from 0 to 3, as said below
- branch_owner: int32 [32], replicated, may hold values from 0 to 3, as said below
- root_pages: int32 [8, 32], replicated, may hold values from 0 to 95, as said below
- branch_pages: int32 [32, 4], replicated, may hold values from 0 to 95, as said below
- root_len: int32 [8], replicated, may hold values from 1 to 4096, as said below
- branch_len: int32 [32], replicated, may hold values from 1 to 512
- leaf_len: int32 [512], P('dp'), may hold values from 1 to 128
- routes: int32 [512, 2], P('dp'), may hold values from 0 to 7, all different within a row; in each aligned block of 128 rows (0 to 127, 128 to 255, ...) at most 64 rows name the same one
Outputs:
- layer_out: bfloat16 [512, 4096], P('dp', 'mp')
The draws below stay inside these ranges and needn't reach their ends.
Inputs may be any that keep to these rules, and one draw needn't show every extreme that they name: `request_branch`: at most 32 requests share a branch, and some branch has exactly 32. `branch_parent`: every root has exactly 4 branches. `root_owner`: every index of dp holds exactly 2 roots. `branch_owner`: every index of dp holds exactly 8 branches. `root_pages`: no slot of an owner's pool serves two pages of its nodes. `branch_pages`: no slot of an owner's pool serves two pages of its nodes. `root_len`: some root has 32 full pages.
All inputs are finite; a program needn't handle non-finite values.
Results may differ from the reference program's by a relative error of at most 0.034.
Values may be sent and summed in bfloat16 or wider, within the bound.
No kernel may reach another device: no remote copies, remote signals or barrier semaphores. Data moves between devices by JAX's collectives and lax.ppermute only.
A program may use at most 576 MiB of HBM per device.

```python
import math
import jax
import jax.numpy as jnp
import numpy as np
from jax import lax

D = 4096
HEADS = 32
KVH = 8
HD = 128
EXPERTS = 8
TOP = 2
FF = 8192
PAGE = 128
R_DEV = 128
ROOT_DEV = 2
ROOT_PG = 32
BR_PG = 4
REQS = 512
ROOTS = 8
BRANCHES = 32
KIDS = 4
BR_CAP = 32
E_CAP = 64
POOL_DEV = 96
POOL = 384
PARTS_SIZE = 1
N_DP = 4


def tree_tables(key):
    table_keys = jax.random.split(jax.random.fold_in(key, 7), 4)
    root_order = jax.random.permutation(table_keys[0], ROOTS)
    branch_order = jax.random.permutation(table_keys[1], BRANCHES)
    parent_order = jax.random.permutation(table_keys[2], BRANCHES)
    pool_orders = jax.vmap(lambda pool_key: jax.random.permutation(pool_key, POOL_DEV))(jax.random.split(table_keys[3], N_DP))
    root_owner = root_order % N_DP
    branch_owner = branch_order % N_DP
    root_slots = (root_order // N_DP)[:, None] * ROOT_PG + jnp.arange(ROOT_PG)[None, :]
    branch_slots = ROOT_DEV * ROOT_PG + (branch_order // N_DP)[:, None] * BR_PG + jnp.arange(BR_PG)[None, :]
    root_pages = pool_orders[root_owner[:, None], root_slots]
    branch_pages = pool_orders[branch_owner[:, None], branch_slots]
    branch_parent = parent_order // KIDS
    return (root_owner, branch_owner, root_pages, branch_pages, branch_parent)


def draw_root_owner(key, part):
    return tree_tables(key)[0].astype(jnp.int32)


def draw_branch_owner(key, part):
    return tree_tables(key)[1].astype(jnp.int32)


def draw_root_pages(key, part):
    return tree_tables(key)[2].astype(jnp.int32)


def draw_branch_pages(key, part):
    return tree_tables(key)[3].astype(jnp.int32)


def draw_branch_parent(key, part):
    return tree_tables(key)[4].astype(jnp.int32)


def draw_request_branch(key, part):
    pick_key, shuffle_key, label_key = jax.random.split(jax.random.fold_in(key, 11), 3)
    spare = BRANCHES * BR_CAP - BR_CAP
    picks = jax.random.permutation(pick_key, spare)[:REQS - BR_CAP] + BR_CAP
    places = jnp.concatenate([jnp.arange(BR_CAP), picks])
    places = jax.random.permutation(shuffle_key, places)
    relabel = jax.random.permutation(label_key, BRANCHES)
    return relabel[places // BR_CAP].astype(jnp.int32)


def draw_root_len(key, part):
    shift_key, cut_key, full_key = jax.random.split(jax.random.fold_in(key, 13), 3)
    longest = ROOT_PG * PAGE
    full_root = jax.random.randint(full_key, (), 0, ROOTS)
    short_root = (full_root + 1) % ROOTS
    shifts = jax.random.randint(shift_key, (ROOTS,), 0, 7)
    shifts = jnp.where(jnp.arange(ROOTS) == short_root, 6, shifts)
    ceiling = jnp.maximum(jnp.right_shift(jnp.full((ROOTS,), longest, jnp.int32), shifts), 1)
    trimmed = jax.random.randint(cut_key, (ROOTS,), 0, ceiling // 2 + 1)
    return jnp.where(jnp.arange(ROOTS) == full_root, longest, ceiling - trimmed).astype(jnp.int32)


def draw_queries(key, part):
    base_key = jax.random.fold_in(key, 0)
    values = 2.0 * jnp.clip(jax.random.normal(base_key, (REQS, HEADS * HD), jnp.float32), -5.0, 5.0)
    return values.astype(jnp.bfloat16)


def draw_residual(key, part):
    column = jnp.arange(D, dtype=jnp.float32) / D
    values = 0.15 * jnp.clip(jax.random.normal(key, (REQS, D), jnp.float32), -5.0, 5.0) * jnp.exp(1.1 * column)[None, :]
    return values.astype(jnp.bfloat16)


def place_ends(array, own_key, smallest, high):
    dims = array.shape
    spot = [jax.random.randint(jax.random.fold_in(own_key, axis), (), 0, dims[axis]) for axis in range(len(dims))]
    array = array.at[tuple(spot)].set(smallest)
    longest = dims.index(max(dims))
    spot[longest] = (spot[longest] + 1) % dims[longest]
    return array.at[tuple(spot)].set(high)


def spiked(result, stream_key, source, target, blocks, factor):
    def block_of(position):
        return (jnp.arange(result.shape[position]) // (result.shape[position] // blocks)).reshape((-1,) + (1,) * (result.ndim - 1 - position))

    near = jax.random.permutation(stream_key, blocks)[block_of(target)]
    far = (block_of(target) + blocks // 2) % blocks
    return jnp.where((block_of(source) == near) | (block_of(source) == far), factor * result, result)


def level_of(stream_key, extent, cuts, smallest, largest):
    factor_of, own = 1.0, jax.random.fold_in(stream_key, 6)
    for dim, blocks in cuts:
        draws = jnp.exp(jax.random.uniform(jax.random.fold_in(own, dim), (blocks,), jnp.float32, smallest / len(cuts), largest / len(cuts)))
        factor_of = factor_of * jnp.repeat(draws, extent[dim] // blocks).reshape([-1 if axis == dim else 1 for axis in range(len(extent))])
    return factor_of


def deal_out(key, own, number, rows, number_of, top, limit, slope):
    order = jax.random.permutation(key, number_of)
    packed, usual = load_shares(number_of, rows * top, limit, slope, True), load_shares(number_of, rows * top, limit, slope, False)
    places = jnp.arange(number_of)

    def named(sizes, offset_by):
        used = int((sizes > 0).sum())
        fixed = max(1, used // 4)
        shifted = fixed + (places - fixed + offset_by * (used - fixed)) % max(1, number_of - fixed)
        return jnp.zeros((number_of,), jnp.int32).at[order[jnp.where(places < fixed, places, shifted)]].set(jnp.asarray(sizes, jnp.int32))

    sizes = jnp.where(number % 4 == 0, named(packed, number // 4), named(usual, number - number // 4 - 1))
    mixed = jax.random.permutation(jax.random.fold_in(own, 3), number_of)
    donor, sink = mixed[0:number_of // 2 * 2:2], mixed[1:number_of // 2 * 2:2]
    slack = jnp.minimum(sizes[donor] - 1, limit - sizes[sink]) // 2
    slack = jnp.where((donor == order[0]) | (sink == order[0]) | (sizes[sink] == 0), 0, jnp.maximum(slack, 0))
    shifted = jax.random.randint(jax.random.fold_in(own, 4), (number_of // 2,), 0, 1 << 20) % (slack + 1)
    sizes = sizes.at[donor].add(-shifted).at[sink].add(shifted)
    members = jnp.searchsorted(jnp.cumsum(sizes), jnp.arange(rows * top), side="right").astype(jnp.int32)
    listing = members.reshape(top, rows).T
    listing = listing[jax.random.permutation(jax.random.fold_in(own, 1), rows)]
    offset_by = jax.random.randint(jax.random.fold_in(own, 2), (rows, 1), 0, top)
    return jnp.take_along_axis(listing, (jnp.arange(top)[None, :] + offset_by) % top, axis=1)


def load_shares(count, total, limit, slope, full):
    loads = [(1 << 20) // math.isqrt(grade ** slope) + 1 for grade in range(1, count + 1)]
    largest = limit if full else min(limit, max(-(-total // count), total * loads[0] // sum(loads)))
    least = 1 if total - largest >= count - 1 else 0
    holding, spare = [largest] + [least] * (count - 1), total - largest - least * (count - 1)
    while spare > 0:
        candidates = [i for i in range(1, count) if holding[i] < largest] or [i for i in range(1, count) if holding[i] < limit]
        pool, remaining = sum([loads[i] for i in candidates]), spare
        for i in candidates:
            more = min(limit - holding[i], max(1, remaining * loads[i] // pool), spare)
            holding[i] = holding[i] + more
            spare = spare - more
    return np.array(holding)


def gaussian(stream_key, extent, deviation, limit, cuts=(), held_as=jnp.bfloat16):
    drawn = jax.random.normal(stream_key, extent, jnp.float32) * deviation
    if len(cuts) > 0:
        drawn = level_of(stream_key, extent, cuts, -0.22, 0.18) * drawn
    return jnp.clip(drawn, min=-limit, max=limit).astype(held_as)


def gaussian_with(own_key, extent, spread, bound, cuts, heavy, held_as=jnp.bfloat16):
    drawn = spread * jax.random.normal(own_key, extent, jnp.float32)
    if cuts:
        drawn = drawn * level_of(own_key, extent, cuts, -0.22, 0.18)
    return jnp.clip(spiked(drawn, jax.random.fold_in(own_key, 3), *heavy), -bound, bound).astype(held_as)


def setup_inputs(seed: int = 0) -> dict:
    streams_of = jax.random.split(jax.random.key(seed), 22)
    queries = draw_queries(jax.random.fold_in(streams_of[21], 71), 0)
    new_kv = gaussian(streams_of[1], (2, REQS, KVH * HD), 1.0, 6.0, ((1, 4),))
    residual = draw_residual(jax.random.fold_in(streams_of[21], 71), 0)
    out_weight = gaussian_with(streams_of[3], (HEADS * HD, D), (HEADS * HD) ** -0.5, 0.125, ((0, 8),), (0, 1, 8, 2.0))
    norm_gain = jnp.clip(1.0 + 0.1 * jax.random.normal(streams_of[4], (D,), jnp.float32), 0.5, 1.5)
    router = gaussian(streams_of[5], (D, EXPERTS), D ** -0.5, 0.09375)
    expert_in = gaussian(streams_of[6], (EXPERTS, 2, FF, D), D ** -0.5, 0.09375, ((0, 4), (2, 8)))
    expert_out = gaussian_with(streams_of[7], (EXPERTS, FF, D), FF ** -0.5, 0.09375, ((0, 4), (1, 8)), (1, 2, 8, 2.0))
    node_cache = gaussian(streams_of[8], (2, POOL, KVH * PARTS_SIZE, PAGE // PARTS_SIZE, HD), 1.0, 6.0, ((1, 4), (2, 8)))
    leaf_cache = gaussian(streams_of[9], (2, REQS, KVH * PARTS_SIZE, PAGE // PARTS_SIZE, HD), 1.0, 6.0, ((1, 4), (2, 8)))
    slot_request = jax.random.permutation(streams_of[10], REQS).astype(jnp.int32)
    request_branch = draw_request_branch(jax.random.fold_in(streams_of[21], 71), 0)
    branch_parent = draw_branch_parent(jax.random.fold_in(streams_of[21], 71), 0)
    root_owner = draw_root_owner(jax.random.fold_in(streams_of[21], 71), 0)
    branch_owner = draw_branch_owner(jax.random.fold_in(streams_of[21], 71), 0)
    root_pages = draw_root_pages(jax.random.fold_in(streams_of[21], 71), 0)
    branch_pages = draw_branch_pages(jax.random.fold_in(streams_of[21], 71), 0)
    root_len = draw_root_len(jax.random.fold_in(streams_of[21], 71), 0)
    branch_len = place_ends(jax.random.randint(streams_of[18], (BRANCHES,), 1, BR_PG * PAGE + 1), jax.random.fold_in(streams_of[18], 1), 1, BR_PG * PAGE).astype(jnp.int32)
    leaf_len = place_ends(jax.random.randint(streams_of[19], (REQS,), 1, PAGE + 1), jax.random.fold_in(streams_of[19], 1), 1, PAGE).astype(jnp.int32)
    routes_keys = jax.random.split(jax.random.fold_in(streams_of[20], 1), REQS // R_DEV)
    routes_turns = jax.random.permutation(jax.random.fold_in(streams_of[20], 3), REQS // R_DEV)
    routes = jax.vmap(lambda own, number: deal_out(jax.random.fold_in(streams_of[20], 2), own, number, R_DEV, EXPERTS, TOP, E_CAP, 2))(routes_keys, routes_turns).reshape((REQS, TOP))
    return {"queries": queries, "new_kv": new_kv, "residual": residual, "out_weight": out_weight, "norm_gain": norm_gain, "router": router, "expert_in": expert_in, "expert_out": expert_out, "node_cache": node_cache, "leaf_cache": leaf_cache, "slot_request": slot_request, "request_branch": request_branch, "branch_parent": branch_parent, "root_owner": root_owner, "branch_owner": branch_owner, "root_pages": root_pages, "branch_pages": branch_pages, "root_len": root_len, "branch_len": branch_len, "leaf_len": leaf_len, "routes": routes}


MASKED_SCORE = -1e+30
NORM_EPS = 1e-05

def rounded(weights):
    return lax.optimization_barrier(weights.astype(jnp.bfloat16)).astype(jnp.float32)

def level_partial(group_queries, key_block, value_block, usable):
    scores = jnp.einsum('ghd,gpld->gphl', group_queries.astype(jnp.float32), key_block.astype(jnp.float32)) * HD ** (-0.5)
    usable = usable[None, :, None, :]
    masked_scores = jnp.where(usable, scores, MASKED_SCORE)
    row_max = lax.optimization_barrier(jnp.max(masked_scores, axis=-1))
    weights = jnp.where(usable, jnp.exp(masked_scores - row_max[..., None]), 0.0)
    weight_total = lax.optimization_barrier(jnp.sum(weights, axis=-1))
    weighted_sum = jnp.einsum('gphl,gpld->gphd', rounded(weights), value_block.astype(jnp.float32))
    return (weighted_sum, row_max, weight_total)

def token_places(page_count):
    token_width = PAGE // PARTS_SIZE
    page_starts = jnp.arange(page_count, dtype=jnp.int32)[:, None] * PAGE
    inside = jnp.arange(token_width, dtype=jnp.int32)[None, :]
    return jnp.stack([(page_starts + part_index * token_width + inside).reshape(-1) for part_index in range(PARTS_SIZE)])

def node_blocks(node_cache, owner, page_list):
    page_ids = (owner * POOL_DEV + page_list).astype(jnp.int32)
    chosen = jnp.take(node_cache, page_ids, axis=1)
    chosen = chosen.reshape(2, page_list.shape[0], KVH, PARTS_SIZE, PAGE // PARTS_SIZE, HD)
    return jnp.transpose(chosen, (0, 2, 3, 1, 4, 5)).reshape(2, KVH, PARTS_SIZE, -1, HD)

def reference(queries, new_kv, residual, out_weight, norm_gain, router, expert_in, expert_out, node_cache, leaf_cache, slot_request, request_branch, branch_parent, root_owner, branch_owner, root_pages, branch_pages, root_len, branch_len, leaf_len, routes):
    requests = queries.shape[0]
    group_size = HEADS // KVH

    def request_output(slot_index):
        request = slot_request[slot_index]
        branch = request_branch[request]
        root_node = branch_parent[branch]
        group_queries = queries[slot_index].reshape(KVH, group_size, HD)
        root_kv = node_blocks(node_cache, root_owner[root_node], root_pages[root_node])
        root_part = level_partial(group_queries, root_kv[0], root_kv[1], token_places(ROOT_PG) < root_len[root_node])
        branch_kv = node_blocks(node_cache, branch_owner[branch], branch_pages[branch])
        branch_part = level_partial(group_queries, branch_kv[0], branch_kv[1], token_places(BR_PG) < branch_len[branch])
        leaf_kv = leaf_cache[:, slot_index].reshape(2, KVH, PARTS_SIZE, PAGE // PARTS_SIZE, HD)
        leaf_part = level_partial(group_queries, leaf_kv[0], leaf_kv[1], token_places(1) < leaf_len[slot_index])
        fresh_keys = new_kv[0, slot_index].reshape(KVH, HD).astype(jnp.float32)
        fresh_values = new_kv[1, slot_index].reshape(KVH, HD).astype(jnp.float32)
        self_score = jnp.einsum('ghd,gd->gh', group_queries.astype(jnp.float32), fresh_keys) * HD ** (-0.5)
        sums = jnp.concatenate([root_part[0], branch_part[0], leaf_part[0]], axis=1)
        maxima = jnp.concatenate([root_part[1], branch_part[1], leaf_part[1]], axis=1)
        totals = jnp.concatenate([root_part[2], branch_part[2], leaf_part[2]], axis=1)
        common_max = jnp.maximum(lax.optimization_barrier(jnp.max(maxima, axis=1)), self_score)
        factors = jnp.exp(maxima - common_max[:, None, :])
        self_factor = jnp.exp(self_score - common_max)
        weighted = lax.optimization_barrier(jnp.sum(sums * factors[..., None], axis=1)) + self_factor[..., None] * fresh_values[:, None, :]
        weight_total = lax.optimization_barrier(jnp.sum(totals * factors, axis=1)) + self_factor
        return (weighted / weight_total[..., None]).reshape(HEADS * HD).astype(jnp.bfloat16)

    def block_output(block_slots):
        return jax.vmap(request_output)(block_slots)
    slot_blocks = jnp.arange(requests, dtype=jnp.int32).reshape(-1, 16)
    attended = lax.map(block_output, slot_blocks).reshape(requests, HEADS * HD)
    attention_out = jnp.dot(attended, out_weight, preferred_element_type=jnp.float32)
    hidden = residual.astype(jnp.float32) + attention_out
    inv_rms = lax.rsqrt(lax.optimization_barrier(jnp.mean(hidden * hidden, axis=1)) + NORM_EPS)
    normed = (hidden * inv_rms[:, None] * norm_gain[None, :]).astype(jnp.bfloat16)
    logits = jnp.dot(normed, router, preferred_element_type=jnp.float32)
    chosen = jnp.take_along_axis(logits, routes, axis=1)
    gate_weights = jax.nn.softmax(chosen, axis=1)
    flat_routes = routes.reshape(-1)
    pair_count = flat_routes.shape[0]
    pair_order = jnp.argsort(flat_routes, stable=True).astype(jnp.int32)
    expert_counts = lax.optimization_barrier(jnp.sum((flat_routes[None, :] == jnp.arange(EXPERTS, dtype=jnp.int32)[:, None]).astype(jnp.int32), axis=1))
    expert_starts = jnp.cumsum(expert_counts) - expert_counts
    capacity = N_DP * E_CAP

    def expert_step(outputs, expert):
        offsets = jnp.arange(capacity, dtype=jnp.int32)
        live = offsets < expert_counts[expert]
        spots = jnp.minimum(expert_starts[expert] + offsets, pair_count - 1).astype(jnp.int32)
        pairs = jnp.where(live, jnp.take(pair_order, spots), pair_count).astype(jnp.int32)
        token_rows = jnp.take(normed, pairs // TOP, axis=0, mode='fill', fill_value=0)
        gate_up = expert_in[expert]
        gate_part = jnp.dot(token_rows, gate_up[0].T, preferred_element_type=jnp.float32)
        up_part = jnp.dot(token_rows, gate_up[1].T, preferred_element_type=jnp.float32)
        expert_hidden = (jax.nn.silu(gate_part) * up_part).astype(jnp.bfloat16)
        expert_result = jnp.dot(expert_hidden, expert_out[expert], preferred_element_type=jnp.float32).astype(jnp.bfloat16)
        return (outputs.at[pairs].set(expert_result, mode='drop'), None)
    outputs, ignored = lax.scan(expert_step, jnp.zeros((pair_count, D), jnp.bfloat16), jnp.arange(EXPERTS, dtype=jnp.int32))
    results = outputs.reshape(requests, TOP, D).astype(jnp.float32)
    layer_out = hidden + lax.optimization_barrier(jnp.sum(gate_weights[:, :, None] * results, axis=1))
    return layer_out.astype(jnp.bfloat16)
```

```python
import jax
import jax.numpy as jnp
from jax import lax
from jax.sharding import PartitionSpec as P

HEADS = 32
KVH = 8
EXPERTS = 8
TOP = 2
PAGE = 128
ROOT_DEV = 2
BR_DEV = 8
BR_CAP = 32
E_CAP = 64


MASKED_SCORE = -1e30
NORM_EPS = 1e-05


def partner(x, axis, apart):
    return lax.ppermute(x, axis, [(i, i ^ 1 << apart) for i in range(lax.axis_size(axis))])


def merge_partials(first_part, second_part):
    first_sum, first_max, first_total = first_part
    second_sum, second_max, second_total = second_part
    common_max = jnp.maximum(first_max, second_max)
    first_factor = jnp.exp(first_max - common_max)
    second_factor = jnp.exp(second_max - common_max)
    merged_sum = first_sum * first_factor[..., None] + second_sum * second_factor[..., None]
    return (merged_sum, common_max, first_total * first_factor + second_total * second_factor)


def weigh_scores(scores, usable, values, pattern):
    masked_scores = jnp.where(usable, scores, MASKED_SCORE)
    row_max = jnp.max(masked_scores, axis=-1)
    weights = jnp.where(usable, jnp.exp(masked_scores - row_max[..., None]), 0.0)
    weight_total = jnp.sum(weights, axis=-1)
    weighted_sum = jnp.einsum(
        pattern, weights.astype(jnp.bfloat16), values, preferred_element_type=jnp.float32
    )
    return (weighted_sum, row_max, weight_total)


def node_partial(all_queries, members, page_pool, page_list, node_length, part_index):
    token_width = page_pool.shape[2]
    head_width = page_pool.shape[3]
    query_rows = jnp.take(all_queries, members, axis=0, mode="fill", fill_value=0)
    node_block = jnp.take(page_pool, page_list, axis=1)
    node_keys = node_block[0].reshape(-1, head_width)
    node_values = node_block[1].reshape(-1, head_width)
    positions = (
        jnp.arange(page_list.shape[0])[:, None] * PAGE
        + part_index * token_width
        + jnp.arange(token_width)[None, :]
    ).reshape(-1)
    usable = (positions < node_length)[None, None, :]
    scores = jnp.einsum(
        "sgd,ld->sgl", query_rows, node_keys, preferred_element_type=jnp.float32
    ) * head_width ** (-0.5)
    return weigh_scores(scores, usable, node_values, "sgl,ld->sgd")


def spread_rows(member_ids, partial_value, requests):
    weighted_sum, row_max, weight_total = partial_value
    flat_ids = member_ids.reshape(-1)
    groups = row_max.shape[-1]
    head_width = weighted_sum.shape[-1]
    sum_rows = (
        jnp.zeros((requests, groups, head_width), jnp.float32)
        .at[flat_ids]
        .set(weighted_sum.reshape(-1, groups, head_width), mode="drop")
    )
    max_rows = (
        jnp.zeros((requests, groups), jnp.float32)
        .at[flat_ids]
        .set(row_max.reshape(-1, groups), mode="drop")
    )
    total_rows = (
        jnp.zeros((requests, groups), jnp.float32)
        .at[flat_ids]
        .set(weight_total.reshape(-1, groups), mode="drop")
    )
    return (sum_rows, max_rows, total_rows)


def shards(
    queries,
    new_kv,
    residual,
    out_weight,
    norm_gain,
    router,
    expert_in,
    expert_out,
    node_cache,
    leaf_cache,
    slot_request,
    request_branch,
    branch_parent,
    root_owner,
    branch_owner,
    root_pages,
    branch_pages,
    root_len,
    branch_len,
    leaf_len,
    routes,
):
    head_width = node_cache.shape[-1]
    token_width = node_cache.shape[-2]
    part_count = lax.axis_size("mp") // KVH
    group_size = HEADS // KVH
    own_heads = HEADS // lax.axis_size("mp")
    local_rows = queries.shape[0]
    requests = slot_request.shape[0]
    branches = branch_parent.shape[0]
    root_count = root_owner.shape[0]
    kid_count = branches // root_count
    mp_index = lax.axis_index("mp")
    dp_index = lax.axis_index("dp")
    kv_head = mp_index // part_count
    part_index = mp_index % part_count
    group_queries = lax.dynamic_slice_in_dim(
        queries, kv_head * group_size * head_width, group_size * head_width, 1
    )
    all_queries = lax.all_gather(group_queries, "dp", axis=0, tiled=True).reshape(
        requests, group_size, head_width
    )
    slot_branch = jnp.take(request_branch, slot_request)
    branch_order = jnp.argsort(slot_branch, stable=True)
    branch_counts = jnp.sum(
        (slot_branch[None, :] == jnp.arange(branches)[:, None]).astype(jnp.int32), axis=1
    )
    branch_starts = jnp.cumsum(branch_counts) - branch_counts
    offsets = jnp.arange(BR_CAP)[None, :]
    spots = jnp.minimum(branch_starts[:, None] + offsets, requests - 1)
    members = jnp.where(offsets < branch_counts[:, None], jnp.take(branch_order, spots), requests)
    kids_of = jnp.argsort(branch_parent, stable=True).reshape(root_count, kid_count)
    page_pool = node_cache[:, :, 0]
    local_roots = jnp.nonzero(root_owner == dp_index, size=ROOT_DEV)[0]
    local_branches = jnp.nonzero(branch_owner == dp_index, size=BR_DEV)[0]

    def root_work(root_node):
        member_ids = jnp.take(members, kids_of[root_node], axis=0).reshape(-1)
        return (
            member_ids,
            node_partial(
                all_queries,
                member_ids,
                page_pool,
                root_pages[root_node],
                root_len[root_node],
                part_index,
            ),
        )

    def branch_work(branch_node):
        member_ids = members[branch_node]
        return (
            member_ids,
            node_partial(
                all_queries,
                member_ids,
                page_pool,
                branch_pages[branch_node],
                branch_len[branch_node],
                part_index,
            ),
        )

    root_ids, root_partial = jax.vmap(root_work)(local_roots)
    branch_ids, branch_partial = jax.vmap(branch_work)(local_branches)
    root_sum, root_max, root_total = spread_rows(root_ids, root_partial, requests)
    branch_sum, branch_max, branch_total = spread_rows(branch_ids, branch_partial, requests)
    groups = root_max.shape[1]
    dp_count = lax.axis_size("dp")

    def stat_row(row_max, row_total):
        stats = jnp.concatenate([row_max, row_total], axis=1)
        return jnp.pad(stats, ((0, 0), (0, head_width - 2 * groups)))[:, None, :]

    packed = jnp.concatenate(
        [root_sum, stat_row(root_max, root_total), branch_sum, stat_row(branch_max, branch_total)],
        axis=1,
    )
    exchanged = lax.all_to_all(
        packed.reshape(dp_count, local_rows, 2 * groups + 2, head_width),
        "dp",
        split_axis=0,
        concat_axis=0,
        tiled=True,
    )
    gathered = jnp.sum(exchanged, axis=0)
    root_stats = gathered[:, groups]
    branch_stats = gathered[:, 2 * groups + 1]
    returned = (
        gathered[:, :groups],
        root_stats[:, :groups],
        root_stats[:, groups : 2 * groups],
        gathered[:, groups + 1 : 2 * groups + 1],
        branch_stats[:, :groups],
        branch_stats[:, groups : 2 * groups],
    )
    leaf_block = leaf_cache[:, :, 0]
    mine_queries = group_queries.reshape(local_rows, group_size, head_width)
    leaf_places = part_index * token_width + jnp.arange(token_width)
    leaf_usable = (leaf_places[None, :] < leaf_len[:, None])[:, None, :]
    leaf_scores = jnp.einsum(
        "rgd,rtd->rgt", mine_queries, leaf_block[0], preferred_element_type=jnp.float32
    ) * head_width ** (-0.5)
    leaf_partial = weigh_scores(leaf_scores, leaf_usable, leaf_block[1], "rgt,rtd->rgd")
    running = merge_partials(
        (returned[0], returned[1], returned[2]), (returned[3], returned[4], returned[5])
    )
    running = merge_partials(running, leaf_partial)
    bit_count = part_count.bit_length() - 1
    for bit_index in reversed(range(bit_count)):
        half_heads = running[1].shape[1] // 2
        upper_side = mp_index >> bit_index & 1 == 1
        kept_half = tuple(
            (
                jnp.where(upper_side, component[:, half_heads:], component[:, :half_heads])
                for component in running
            )
        )
        sent_half = tuple(
            (
                jnp.where(upper_side, component[:, :half_heads], component[:, half_heads:])
                for component in running
            )
        )
        received = partner((sent_half[0], sent_half[1], sent_half[2]), "mp", bit_index)
        running = merge_partials(kept_half, received)
    own_queries = lax.dynamic_slice_in_dim(
        queries, mp_index * own_heads * head_width, own_heads * head_width, 1
    ).reshape(local_rows, own_heads, head_width)
    fresh_kv = lax.dynamic_slice_in_dim(new_kv, kv_head * head_width, head_width, 2)
    self_score = jnp.einsum(
        "rhd,rd->rh", own_queries, fresh_kv[0], preferred_element_type=jnp.float32
    ) * head_width ** (-0.5)
    weighted, row_max, weight_total = running
    common_max = jnp.maximum(row_max, self_score)
    old_factor = jnp.exp(row_max - common_max)
    new_factor = jnp.exp(self_score - common_max)
    weighted = (
        weighted * old_factor[..., None]
        + new_factor[..., None] * fresh_kv[1].astype(jnp.float32)[:, None, :]
    )
    weight_total = weight_total * old_factor + new_factor
    attended = (
        (weighted / weight_total[..., None])
        .astype(jnp.bfloat16)
        .reshape(local_rows, own_heads * head_width)
    )
    projected = jnp.dot(attended, out_weight, preferred_element_type=jnp.float32)
    slice_width = residual.shape[1]
    start_col = mp_index * slice_width
    own_cols = lax.dynamic_slice_in_dim(projected, start_col, slice_width, 1) + residual.astype(
        jnp.float32
    )
    projected = lax.dynamic_update_slice_in_dim(projected, own_cols, start_col, 1)
    hidden = lax.psum(projected.astype(jnp.bfloat16), "mp").astype(jnp.float32)
    inv_rms = lax.rsqrt(jnp.mean(hidden * hidden, axis=1) + NORM_EPS)
    normed = (hidden * inv_rms[:, None] * norm_gain[None, :]).astype(jnp.bfloat16)
    kept_cols = lax.dynamic_slice_in_dim(hidden, start_col, slice_width, 1)
    logits = jnp.dot(normed, router, preferred_element_type=jnp.float32)
    route_hits = routes[:, :, None] == jnp.arange(EXPERTS)[None, None, :]
    chosen = jnp.sum(jnp.where(route_hits, logits[:, None, :], 0.0), axis=2)
    gate_weights = jax.nn.softmax(chosen, axis=1)
    pair_experts = routes.reshape(-1)
    pair_onehot = (pair_experts[:, None] == jnp.arange(EXPERTS)[None, :]).astype(jnp.int32)
    pair_rank = jnp.sum((jnp.cumsum(pair_onehot, axis=0) - 1) * pair_onehot, axis=1)
    pair_slot = pair_experts * E_CAP + pair_rank
    slot_source = (
        jnp.full((EXPERTS * E_CAP,), local_rows, jnp.int32)
        .at[pair_slot]
        .set(jnp.arange(pair_experts.shape[0], dtype=jnp.int32) // TOP)
    )
    padded = jnp.concatenate([normed, jnp.zeros((1, normed.shape[1]), jnp.bfloat16)], axis=0)
    local_experts = expert_in.shape[0]
    outgoing = jnp.take(padded, slot_source, axis=0).reshape(
        dp_count, local_experts * E_CAP, normed.shape[1]
    )
    incoming = lax.all_to_all(outgoing, "dp", split_axis=0, concat_axis=0, tiled=True).reshape(
        dp_count, local_experts, E_CAP, normed.shape[1]
    )
    gate_up = jnp.einsum(
        "sjcd,jkfd->ksjcf", incoming, expert_in, preferred_element_type=jnp.float32
    )
    expert_hidden = (jax.nn.silu(gate_up[0]) * gate_up[1]).astype(jnp.bfloat16)
    expert_partial = jnp.einsum(
        "sjcf,jfd->sjcd", expert_hidden, expert_out, preferred_element_type=jnp.float32
    )
    summed = lax.psum_scatter(
        expert_partial.astype(jnp.bfloat16), "mp", scatter_dimension=3, tiled=True
    )
    returned_rows = lax.all_to_all(
        summed.reshape(dp_count, local_experts * E_CAP, slice_width),
        "dp",
        split_axis=0,
        concat_axis=0,
        tiled=True,
    )
    results = jnp.take(returned_rows.reshape(-1, slice_width), pair_slot, axis=0).reshape(
        local_rows, TOP, slice_width
    )
    layer_out = kept_cols + jnp.sum(gate_weights[:, :, None] * results.astype(jnp.float32), axis=1)
    return layer_out.astype(jnp.bfloat16)


def solution(mesh):
    placed = (
        P("dp", None),
        P(None, "dp", None),
        P("dp", "mp"),
        P("mp", None),
        P(),
        P(),
        P("dp", None, "mp", None),
        P("dp", "mp", None),
        P(None, "dp", "mp", None, None),
        P(None, "dp", "mp", None, None),
        P(),
        P(),
        P(),
        P(),
        P(),
        P(),
        P(),
        P(),
        P(),
        P("dp"),
        P("dp", None),
    )
    return jax.shard_map(
        shards, mesh=mesh, in_specs=placed, out_specs=P("dp", "mp"), check_vma=False
    )
```

```python
import jax
import jax.numpy as jnp
from jax import lax
from jax.sharding import PartitionSpec as P

HEADS = 32
KVH = 8
EXPERTS = 8
TOP = 2
PAGE = 128
ROOT_DEV = 2
BR_DEV = 8
BR_CAP = 32
E_CAP = 64


MASKED_SCORE = -1e30
NORM_EPS = 1e-05


def partner(x, axis, apart):
    return lax.ppermute(x, axis, [(i, i ^ 1 << apart) for i in range(lax.axis_size(axis))])


def merge_partials(first_part, second_part):
    first_sum, first_max, first_total = first_part
    second_sum, second_max, second_total = second_part
    common_max = jnp.maximum(first_max, second_max)
    first_factor = jnp.exp(first_max - common_max)
    second_factor = jnp.exp(second_max - common_max)
    merged_sum = first_sum * first_factor[..., None] + second_sum * second_factor[..., None]
    return (merged_sum, common_max, first_total * first_factor + second_total * second_factor)


def weigh_scores(scores, usable, values, pattern):
    masked_scores = jnp.where(usable, scores, MASKED_SCORE)
    row_max = jnp.max(masked_scores, axis=-1)
    weights = jnp.where(usable, jnp.exp(masked_scores - row_max[..., None]), 0.0)
    weight_total = jnp.sum(weights, axis=-1)
    weighted_sum = jnp.einsum(
        pattern, weights.astype(jnp.bfloat16), values, preferred_element_type=jnp.float32
    )
    return (weighted_sum, row_max, weight_total)


def shards(
    queries,
    new_kv,
    residual,
    out_weight,
    norm_gain,
    router,
    expert_in,
    expert_out,
    node_cache,
    leaf_cache,
    slot_request,
    request_branch,
    branch_parent,
    root_owner,
    branch_owner,
    root_pages,
    branch_pages,
    root_len,
    branch_len,
    leaf_len,
    routes,
):
    head_width = node_cache.shape[-1]
    token_width = node_cache.shape[-2]
    part_count = lax.axis_size("mp") // KVH
    group_size = HEADS // KVH
    own_heads = HEADS // lax.axis_size("mp")
    local_rows = queries.shape[0]
    requests = slot_request.shape[0]
    branches = branch_parent.shape[0]
    root_count = root_owner.shape[0]
    mp_index = lax.axis_index("mp")
    dp_index = lax.axis_index("dp")
    kv_head = mp_index // part_count
    part_index = mp_index % part_count
    group_queries = lax.dynamic_slice_in_dim(
        queries, kv_head * group_size * head_width, group_size * head_width, 1
    )
    all_queries = lax.all_gather(group_queries, "dp", axis=0, tiled=True).reshape(
        requests, group_size, head_width
    )
    slot_branch = jnp.take(request_branch, slot_request)
    slot_root = jnp.take(branch_parent, slot_branch)
    local_roots = jnp.nonzero(root_owner == dp_index, size=ROOT_DEV)[0]
    local_branches = jnp.nonzero(branch_owner == dp_index, size=BR_DEV)[0]
    page_pool = node_cache[:, :, 0]
    pool_pages = page_pool.shape[1]
    flat_queries = all_queries.reshape(requests, group_size * head_width)

    def selection(node_of_slot, nodes, cap):
        hit = node_of_slot[None, :] == nodes[:, None]
        rank = jnp.cumsum(hit.astype(jnp.int32), axis=1) - 1
        return hit[:, None, :] & (rank[:, None, :] == jnp.arange(cap)[None, :, None])

    def level_rows(nodes, node_pages, node_len, cap):
        pick = selection(node_of_slot_for[cap], nodes, cap)
        member_queries = jnp.einsum(
            "nks,sx->nkx", pick.astype(jnp.bfloat16), flat_queries,
            preferred_element_type=jnp.float32,
        ).astype(jnp.bfloat16).reshape(nodes.shape[0], cap, group_size, head_width)
        page_pick = (
            jnp.take(node_pages, nodes, axis=0)[:, :, None] == jnp.arange(pool_pages)[None, None, :]
        ).astype(jnp.bfloat16)
        blocks = jnp.einsum(
            "npq,cqtd->cnptd", page_pick, page_pool, preferred_element_type=jnp.float32
        ).astype(jnp.bfloat16)
        lengths = jnp.take(node_len, nodes)

        def one_node(queries_of, keys_of, values_of, length):
            page_count = keys_of.shape[0]
            positions = (
                jnp.arange(page_count)[:, None] * PAGE
                + part_index * token_width
                + jnp.arange(token_width)[None, :]
            ).reshape(-1)
            usable = (positions < length)[None, None, :]
            scores = jnp.einsum(
                "sgd,ld->sgl", queries_of, keys_of.reshape(-1, head_width),
                preferred_element_type=jnp.float32,
            ) * head_width ** (-0.5)
            return weigh_scores(scores, usable, values_of.reshape(-1, head_width), "sgl,ld->sgd")

        weighted_sum, row_max, weight_total = jax.vmap(one_node)(
            member_queries, blocks[0], blocks[1], lengths
        )
        stats = jnp.concatenate([row_max, weight_total], axis=2)
        stats = jnp.pad(stats, ((0, 0), (0, 0), (0, head_width - 2 * group_size)))
        rows = jnp.concatenate(
            [weighted_sum.reshape(nodes.shape[0], cap, group_size * head_width), stats], axis=2
        )
        return jnp.einsum(
            "nks,nkc->sc", pick.astype(jnp.float32), rows,
            precision=lax.Precision.HIGHEST, preferred_element_type=jnp.float32,
        )

    root_cap = (branches // root_count) * BR_CAP
    node_of_slot_for = {root_cap: slot_root, BR_CAP: slot_branch}
    root_rows = level_rows(local_roots, root_pages, root_len, root_cap)
    branch_rows = level_rows(local_branches, branch_pages, branch_len, BR_CAP)
    groups = group_size
    dp_count = lax.axis_size("dp")
    packed = jnp.concatenate([root_rows, branch_rows], axis=1)
    exchanged = lax.all_to_all(
        packed.reshape(dp_count, local_rows, 2 * groups + 2, head_width),
        "dp",
        split_axis=0,
        concat_axis=0,
        tiled=True,
    )
    gathered = jnp.sum(exchanged, axis=0)
    root_stats = gathered[:, groups]
    branch_stats = gathered[:, 2 * groups + 1]
    returned = (
        gathered[:, :groups],
        root_stats[:, :groups],
        root_stats[:, groups : 2 * groups],
        gathered[:, groups + 1 : 2 * groups + 1],
        branch_stats[:, :groups],
        branch_stats[:, groups : 2 * groups],
    )
    leaf_block = leaf_cache[:, :, 0]
    mine_queries = group_queries.reshape(local_rows, group_size, head_width)
    leaf_places = part_index * token_width + jnp.arange(token_width)
    leaf_usable = (leaf_places[None, :] < leaf_len[:, None])[:, None, :]
    leaf_scores = jnp.einsum(
        "rgd,rtd->rgt", mine_queries, leaf_block[0], preferred_element_type=jnp.float32
    ) * head_width ** (-0.5)
    leaf_partial = weigh_scores(leaf_scores, leaf_usable, leaf_block[1], "rgt,rtd->rgd")
    running = merge_partials(
        (returned[0], returned[1], returned[2]), (returned[3], returned[4], returned[5])
    )
    running = merge_partials(running, leaf_partial)
    bit_count = part_count.bit_length() - 1
    for bit_index in reversed(range(bit_count)):
        half_heads = running[1].shape[1] // 2
        upper_side = mp_index >> bit_index & 1 == 1
        kept_half = tuple(
            (
                jnp.where(upper_side, component[:, half_heads:], component[:, :half_heads])
                for component in running
            )
        )
        sent_half = tuple(
            (
                jnp.where(upper_side, component[:, :half_heads], component[:, half_heads:])
                for component in running
            )
        )
        received = partner((sent_half[0], sent_half[1], sent_half[2]), "mp", bit_index)
        running = merge_partials(kept_half, received)
    own_queries = lax.dynamic_slice_in_dim(
        queries, mp_index * own_heads * head_width, own_heads * head_width, 1
    ).reshape(local_rows, own_heads, head_width)
    fresh_kv = lax.dynamic_slice_in_dim(new_kv, kv_head * head_width, head_width, 2)
    self_score = jnp.einsum(
        "rhd,rd->rh", own_queries, fresh_kv[0], preferred_element_type=jnp.float32
    ) * head_width ** (-0.5)
    weighted, row_max, weight_total = running
    common_max = jnp.maximum(row_max, self_score)
    old_factor = jnp.exp(row_max - common_max)
    new_factor = jnp.exp(self_score - common_max)
    weighted = (
        weighted * old_factor[..., None]
        + new_factor[..., None] * fresh_kv[1].astype(jnp.float32)[:, None, :]
    )
    weight_total = weight_total * old_factor + new_factor
    attended = (
        (weighted / weight_total[..., None])
        .astype(jnp.bfloat16)
        .reshape(local_rows, own_heads * head_width)
    )
    projected = jnp.dot(attended, out_weight, preferred_element_type=jnp.float32)
    slice_width = residual.shape[1]
    mp_count = lax.axis_size("mp")
    start_col = mp_index * slice_width
    own_cols = lax.dynamic_slice_in_dim(projected, start_col, slice_width, 1) + residual.astype(
        jnp.float32
    )
    projected = lax.dynamic_update_slice_in_dim(projected, own_cols, start_col, 1)
    terms = projected.astype(jnp.bfloat16).reshape(local_rows, mp_count, slice_width)
    terms = jnp.transpose(terms, (1, 0, 2))
    received_terms = lax.all_to_all(terms, "mp", split_axis=0, concat_axis=0, tiled=True)
    kept_cols = jnp.sum(received_terms.astype(jnp.float32), axis=0)
    spread_cols = jnp.broadcast_to(
        kept_cols.astype(jnp.bfloat16)[None], (mp_count, local_rows, slice_width)
    )
    all_cols = lax.all_to_all(spread_cols, "mp", split_axis=0, concat_axis=0, tiled=True)
    hidden = jnp.transpose(all_cols, (1, 0, 2)).reshape(local_rows, -1).astype(jnp.float32)
    inv_rms = lax.rsqrt(jnp.mean(hidden * hidden, axis=1) + NORM_EPS)
    normed = (hidden * inv_rms[:, None] * norm_gain[None, :]).astype(jnp.bfloat16)
    logits = jnp.dot(normed, router, preferred_element_type=jnp.float32)
    route_hits = routes[:, :, None] == jnp.arange(EXPERTS)[None, None, :]
    chosen = jnp.sum(jnp.where(route_hits, logits[:, None, :], 0.0), axis=2)
    gate_weights = jax.nn.softmax(chosen, axis=1)
    pair_experts = routes.reshape(-1)
    pair_onehot = (pair_experts[:, None] == jnp.arange(EXPERTS)[None, :]).astype(jnp.int32)
    pair_rank = jnp.sum((jnp.cumsum(pair_onehot, axis=0) - 1) * pair_onehot, axis=1)
    pair_slot = pair_experts * E_CAP + pair_rank
    slot_source = (
        jnp.full((EXPERTS * E_CAP,), local_rows, jnp.int32)
        .at[pair_slot]
        .set(jnp.arange(pair_experts.shape[0], dtype=jnp.int32) // TOP)
    )
    padded = jnp.concatenate([normed, jnp.zeros((1, normed.shape[1]), jnp.bfloat16)], axis=0)
    local_experts = expert_in.shape[0]
    outgoing = jnp.take(padded, slot_source, axis=0).reshape(
        dp_count, local_experts * E_CAP, normed.shape[1]
    )
    incoming = lax.all_to_all(outgoing, "dp", split_axis=0, concat_axis=0, tiled=True).reshape(
        dp_count, local_experts, E_CAP, normed.shape[1]
    )
    gate_up = jnp.einsum(
        "sjcd,jkfd->ksjcf", incoming, expert_in, preferred_element_type=jnp.float32
    )
    expert_hidden = (jax.nn.silu(gate_up[0]) * gate_up[1]).astype(jnp.bfloat16)
    expert_partial = jnp.einsum(
        "sjcf,jfd->sjcd", expert_hidden, expert_out, preferred_element_type=jnp.float32
    )
    summed = lax.psum_scatter(
        expert_partial.astype(jnp.bfloat16), "mp", scatter_dimension=3, tiled=True
    )
    returned_rows = lax.all_to_all(
        summed.reshape(dp_count, local_experts * E_CAP, slice_width),
        "dp",
        split_axis=0,
        concat_axis=0,
        tiled=True,
    )
    results = jnp.take(returned_rows.reshape(-1, slice_width), pair_slot, axis=0).reshape(
        local_rows, TOP, slice_width
    )
    layer_out = kept_cols + jnp.sum(gate_weights[:, :, None] * results.astype(jnp.float32), axis=1)
    return layer_out.astype(jnp.bfloat16)


def solution(mesh):
    placed = (
        P("dp", None),
        P(None, "dp", None),
        P("dp", "mp"),
        P("mp", None),
        P(),
        P(),
        P("dp", None, "mp", None),
        P("dp", "mp", None),
        P(None, "dp", "mp", None, None),
        P(None, "dp", "mp", None, None),
        P(),
        P(),
        P(),
        P(),
        P(),
        P(),
        P(),
        P(),
        P(),
        P("dp"),
        P("dp", None),
    )
    return jax.shard_map(
        shards, mesh=mesh, in_specs=placed, out_specs=P("dp", "mp"), check_vma=False
    )
```

```python
import jax
import jax.numpy as jnp
from jax import lax
from jax.sharding import PartitionSpec as P

HEADS = 32
KVH = 8
EXPERTS = 8
TOP = 2
PAGE = 128
ROOT_DEV = 2
BR_DEV = 8
BR_CAP = 32
E_CAP = 64


MASKED_SCORE = -1e30
NORM_EPS = 1e-05


def partner(x, axis, apart):
    return lax.ppermute(x, axis, [(i, i ^ 1 << apart) for i in range(lax.axis_size(axis))])


def merge_partials(first_part, second_part):
    first_sum, first_max, first_total = first_part
    second_sum, second_max, second_total = second_part
    common_max = jnp.maximum(first_max, second_max)
    first_factor = jnp.exp(first_max - common_max)
    second_factor = jnp.exp(second_max - common_max)
    merged_sum = first_sum * first_factor[..., None] + second_sum * second_factor[..., None]
    return (merged_sum, common_max, first_total * first_factor + second_total * second_factor)


def weigh_scores(scores, usable, values, pattern):
    masked_scores = jnp.where(usable, scores, MASKED_SCORE)
    row_max = jnp.max(masked_scores, axis=-1)
    weights = jnp.where(usable, jnp.exp(masked_scores - row_max[..., None]), 0.0)
    weight_total = jnp.sum(weights, axis=-1)
    weighted_sum = jnp.einsum(
        pattern, weights.astype(jnp.bfloat16), values, preferred_element_type=jnp.float32
    )
    return (weighted_sum, row_max, weight_total)


def shards(
    queries,
    new_kv,
    residual,
    out_weight,
    norm_gain,
    router,
    expert_in,
    expert_out,
    node_cache,
    leaf_cache,
    slot_request,
    request_branch,
    branch_parent,
    root_owner,
    branch_owner,
    root_pages,
    branch_pages,
    root_len,
    branch_len,
    leaf_len,
    routes,
):
    head_width = node_cache.shape[-1]
    token_width = node_cache.shape[-2]
    part_count = lax.axis_size("mp") // KVH
    group_size = HEADS // KVH
    own_heads = HEADS // lax.axis_size("mp")
    local_rows = queries.shape[0]
    requests = slot_request.shape[0]
    branches = branch_parent.shape[0]
    root_count = root_owner.shape[0]
    mp_index = lax.axis_index("mp")
    dp_index = lax.axis_index("dp")
    kv_head = mp_index // part_count
    part_index = mp_index % part_count
    group_queries = lax.dynamic_slice_in_dim(
        queries, kv_head * group_size * head_width, group_size * head_width, 1
    )
    all_queries = lax.all_gather(group_queries, "dp", axis=0, tiled=True).reshape(
        requests, group_size, head_width
    )
    slot_branch = jnp.sum(
        jnp.where(
            slot_request[:, None] == jnp.arange(requests)[None, :], request_branch[None, :], 0
        ),
        axis=1,
    )
    slot_root = jnp.sum(
        jnp.where(
            slot_branch[:, None] == jnp.arange(branches)[None, :], branch_parent[None, :], 0
        ),
        axis=1,
    )
    local_roots = jnp.nonzero(root_owner == dp_index, size=ROOT_DEV)[0]
    local_branches = jnp.nonzero(branch_owner == dp_index, size=BR_DEV)[0]
    page_pool = node_cache[:, :, 0]
    pool_pages = page_pool.shape[1]
    flat_queries = all_queries.reshape(requests, group_size * head_width)

    def selection(node_of_slot, nodes, cap):
        hit = node_of_slot[None, :] == nodes[:, None]
        rank = jnp.cumsum(hit.astype(jnp.int32), axis=1) - 1
        return hit[:, None, :] & (rank[:, None, :] == jnp.arange(cap)[None, :, None])

    def level_rows(nodes, node_pages, node_len, cap):
        pick = selection(node_of_slot_for[cap], nodes, cap)
        member_queries = jnp.einsum(
            "nks,sx->nkx", pick.astype(jnp.bfloat16), flat_queries,
            preferred_element_type=jnp.float32,
        ).astype(jnp.bfloat16).reshape(nodes.shape[0], cap, group_size, head_width)
        page_pick = (
            jnp.take(node_pages, nodes, axis=0)[:, :, None] == jnp.arange(pool_pages)[None, None, :]
        ).astype(jnp.bfloat16)
        blocks = jnp.einsum(
            "npq,cqtd->cnptd", page_pick, page_pool, preferred_element_type=jnp.float32
        ).astype(jnp.bfloat16)
        lengths = jnp.take(node_len, nodes)

        def one_node(queries_of, keys_of, values_of, length):
            page_count = keys_of.shape[0]
            positions = (
                jnp.arange(page_count)[:, None] * PAGE
                + part_index * token_width
                + jnp.arange(token_width)[None, :]
            ).reshape(-1)
            usable = (positions < length)[None, None, :]
            scores = jnp.einsum(
                "sgd,ld->sgl", queries_of, keys_of.reshape(-1, head_width),
                preferred_element_type=jnp.float32,
            ) * head_width ** (-0.5)
            return weigh_scores(scores, usable, values_of.reshape(-1, head_width), "sgl,ld->sgd")

        weighted_sum, row_max, weight_total = jax.vmap(one_node)(
            member_queries, blocks[0], blocks[1], lengths
        )
        stats = jnp.concatenate([row_max, weight_total], axis=2)
        stats = jnp.pad(stats, ((0, 0), (0, 0), (0, head_width - 2 * group_size)))
        rows = jnp.concatenate(
            [weighted_sum.reshape(nodes.shape[0], cap, group_size * head_width), stats], axis=2
        )
        return jnp.einsum(
            "nks,nkc->sc", pick.astype(jnp.float32), rows,
            precision=lax.Precision.HIGHEST, preferred_element_type=jnp.float32,
        )

    root_cap = (branches // root_count) * BR_CAP
    node_of_slot_for = {root_cap: slot_root, BR_CAP: slot_branch}
    root_rows = level_rows(local_roots, root_pages, root_len, root_cap)
    branch_rows = level_rows(local_branches, branch_pages, branch_len, BR_CAP)
    groups = group_size
    dp_count = lax.axis_size("dp")
    packed = jnp.concatenate([root_rows, branch_rows], axis=1)
    exchanged = lax.all_to_all(
        packed.reshape(dp_count, local_rows, (2 * groups + 2) * head_width),
        "dp",
        split_axis=0,
        concat_axis=0,
        tiled=True,
    )
    gathered = jnp.sum(exchanged, axis=0).reshape(local_rows, 2 * groups + 2, head_width)
    root_stats = gathered[:, groups]
    branch_stats = gathered[:, 2 * groups + 1]
    returned = (
        gathered[:, :groups],
        root_stats[:, :groups],
        root_stats[:, groups : 2 * groups],
        gathered[:, groups + 1 : 2 * groups + 1],
        branch_stats[:, :groups],
        branch_stats[:, groups : 2 * groups],
    )
    leaf_block = leaf_cache[:, :, 0]
    mine_queries = group_queries.reshape(local_rows, group_size, head_width)
    leaf_places = part_index * token_width + jnp.arange(token_width)
    leaf_usable = (leaf_places[None, :] < leaf_len[:, None])[:, None, :]
    leaf_scores = jnp.einsum(
        "rgd,rtd->rgt", mine_queries, leaf_block[0], preferred_element_type=jnp.float32
    ) * head_width ** (-0.5)
    leaf_partial = weigh_scores(leaf_scores, leaf_usable, leaf_block[1], "rgt,rtd->rgd")
    running = merge_partials(
        (returned[0], returned[1], returned[2]), (returned[3], returned[4], returned[5])
    )
    running = merge_partials(running, leaf_partial)
    bit_count = part_count.bit_length() - 1
    for bit_index in reversed(range(bit_count)):
        half_heads = running[1].shape[1] // 2
        upper_side = mp_index >> bit_index & 1 == 1
        kept_half = tuple(
            (
                jnp.where(upper_side, component[:, half_heads:], component[:, :half_heads])
                for component in running
            )
        )
        sent_half = tuple(
            (
                jnp.where(upper_side, component[:, :half_heads], component[:, half_heads:])
                for component in running
            )
        )
        received = partner((sent_half[0], sent_half[1], sent_half[2]), "mp", bit_index)
        running = merge_partials(kept_half, received)
    own_queries = lax.dynamic_slice_in_dim(
        queries, mp_index * own_heads * head_width, own_heads * head_width, 1
    ).reshape(local_rows, own_heads, head_width)
    fresh_kv = lax.dynamic_slice_in_dim(new_kv, kv_head * head_width, head_width, 2)
    self_score = jnp.einsum(
        "rhd,rd->rh", own_queries, fresh_kv[0], preferred_element_type=jnp.float32
    ) * head_width ** (-0.5)
    weighted, row_max, weight_total = running
    common_max = jnp.maximum(row_max, self_score)
    old_factor = jnp.exp(row_max - common_max)
    new_factor = jnp.exp(self_score - common_max)
    weighted = (
        weighted * old_factor[..., None]
        + new_factor[..., None] * fresh_kv[1].astype(jnp.float32)[:, None, :]
    )
    weight_total = weight_total * old_factor + new_factor
    attended = (
        (weighted / weight_total[..., None])
        .astype(jnp.bfloat16)
        .reshape(local_rows, own_heads * head_width)
    )
    projected = jnp.dot(attended, out_weight, preferred_element_type=jnp.float32)
    slice_width = residual.shape[1]
    mp_count = lax.axis_size("mp")
    start_col = mp_index * slice_width
    own_cols = lax.dynamic_slice_in_dim(projected, start_col, slice_width, 1) + residual.astype(
        jnp.float32
    )
    projected = lax.dynamic_update_slice_in_dim(projected, own_cols, start_col, 1)
    terms = projected.astype(jnp.bfloat16).reshape(local_rows, mp_count, slice_width)
    terms = jnp.transpose(terms, (1, 0, 2))
    received_terms = lax.all_to_all(terms, "mp", split_axis=0, concat_axis=0, tiled=True)
    kept_cols = jnp.sum(received_terms.astype(jnp.float32), axis=0)
    spread_cols = jnp.broadcast_to(
        kept_cols.astype(jnp.bfloat16)[None], (mp_count, local_rows, slice_width)
    )
    all_cols = lax.all_to_all(spread_cols, "mp", split_axis=0, concat_axis=0, tiled=True)
    hidden = jnp.transpose(all_cols, (1, 0, 2)).reshape(local_rows, -1).astype(jnp.float32)
    inv_rms = lax.rsqrt(jnp.mean(hidden * hidden, axis=1) + NORM_EPS)
    normed = (hidden * inv_rms[:, None] * norm_gain[None, :]).astype(jnp.bfloat16)
    logits = jnp.dot(normed, router, preferred_element_type=jnp.float32)
    route_hits = routes[:, :, None] == jnp.arange(EXPERTS)[None, None, :]
    chosen = jnp.sum(jnp.where(route_hits, logits[:, None, :], 0.0), axis=2)
    gate_weights = jax.nn.softmax(chosen, axis=1)
    pair_experts = routes.reshape(-1)
    pair_onehot = (pair_experts[:, None] == jnp.arange(EXPERTS)[None, :]).astype(jnp.int32)
    pair_rank = jnp.sum((jnp.cumsum(pair_onehot, axis=0) - 1) * pair_onehot, axis=1)
    pair_slot = pair_experts * E_CAP + pair_rank
    slot_source = (
        jnp.full((EXPERTS * E_CAP,), local_rows, jnp.int32)
        .at[pair_slot]
        .set(jnp.arange(pair_experts.shape[0], dtype=jnp.int32) // TOP)
    )
    padded = jnp.concatenate([normed, jnp.zeros((1, normed.shape[1]), jnp.bfloat16)], axis=0)
    local_experts = expert_in.shape[0]
    outgoing = jnp.take(padded, slot_source, axis=0).reshape(
        dp_count, local_experts, E_CAP, normed.shape[1]
    )
    returned_parts = []
    for expert_index in range(local_experts):
        incoming = lax.all_to_all(
            outgoing[:, expert_index], "dp", split_axis=0, concat_axis=0, tiled=True
        )
        gate_up = jnp.einsum(
            "scd,kfd->kscf", incoming, expert_in[expert_index], preferred_element_type=jnp.float32
        )
        expert_hidden = (jax.nn.silu(gate_up[0]) * gate_up[1]).astype(jnp.bfloat16)
        expert_partial = jnp.einsum(
            "scf,fd->scd", expert_hidden, expert_out[expert_index],
            preferred_element_type=jnp.float32,
        )
        summed = lax.psum_scatter(
            expert_partial.astype(jnp.bfloat16), "mp", scatter_dimension=2, tiled=True
        )
        returned_parts.append(
            lax.all_to_all(summed, "dp", split_axis=0, concat_axis=0, tiled=True)
        )
    returned_rows = jnp.stack(returned_parts, axis=1)
    results = jnp.take(returned_rows.reshape(-1, slice_width), pair_slot, axis=0).reshape(
        local_rows, TOP, slice_width
    )
    layer_out = kept_cols + jnp.sum(gate_weights[:, :, None] * results.astype(jnp.float32), axis=1)
    return layer_out.astype(jnp.bfloat16)


def solution(mesh):
    placed = (
        P("dp", None),
        P(None, "dp", None),
        P("dp", "mp"),
        P("mp", None),
        P(),
        P(),
        P("dp", None, "mp", None),
        P("dp", "mp", None),
        P(None, "dp", "mp", None, None),
        P(None, "dp", "mp", None, None),
        P(),
        P(),
        P(),
        P(),
        P(),
        P(),
        P(),
        P(),
        P(),
        P("dp"),
        P("dp", None),
    )
    return jax.shard_map(
        shards, mesh=mesh, in_specs=placed, out_specs=P("dp", "mp"), check_vma=False
    )
```

```python
import jax
import jax.numpy as jnp
from jax import lax
from jax.sharding import PartitionSpec as P

HEADS = 32
KVH = 8
EXPERTS = 8
TOP = 2
PAGE = 128
ROOT_DEV = 2
BR_DEV = 8
BR_CAP = 32
E_CAP = 64


MASKED_SCORE = -1e30
NORM_EPS = 1e-05


def partner(x, axis, apart):
    return lax.ppermute(x, axis, [(i, i ^ 1 << apart) for i in range(lax.axis_size(axis))])


def merge_partials(first_part, second_part):
    first_sum, first_max, first_total = first_part
    second_sum, second_max, second_total = second_part
    common_max = jnp.maximum(first_max, second_max)
    first_factor = jnp.exp(first_max - common_max)
    second_factor = jnp.exp(second_max - common_max)
    merged_sum = first_sum * first_factor[..., None] + second_sum * second_factor[..., None]
    return (merged_sum, common_max, first_total * first_factor + second_total * second_factor)


def weigh_scores(scores, usable, values, pattern):
    masked_scores = jnp.where(usable, scores, MASKED_SCORE)
    row_max = jnp.max(masked_scores, axis=-1)
    weights = jnp.where(usable, jnp.exp(masked_scores - row_max[..., None]), 0.0)
    weight_total = jnp.sum(weights, axis=-1)
    weighted_sum = jnp.einsum(
        pattern, weights.astype(jnp.bfloat16), values, preferred_element_type=jnp.float32
    )
    return (weighted_sum, row_max, weight_total)


def shards(
    queries,
    new_kv,
    residual,
    out_weight,
    norm_gain,
    router,
    expert_in,
    expert_out,
    node_cache,
    leaf_cache,
    slot_request,
    request_branch,
    branch_parent,
    root_owner,
    branch_owner,
    root_pages,
    branch_pages,
    root_len,
    branch_len,
    leaf_len,
    routes,
):
    head_width = node_cache.shape[-1]
    token_width = node_cache.shape[-2]
    part_count = lax.axis_size("mp") // KVH
    group_size = HEADS // KVH
    own_heads = HEADS // lax.axis_size("mp")
    local_rows = queries.shape[0]
    requests = slot_request.shape[0]
    branches = branch_parent.shape[0]
    root_count = root_owner.shape[0]
    mp_index = lax.axis_index("mp")
    dp_index = lax.axis_index("dp")
    kv_head = mp_index // part_count
    part_index = mp_index % part_count
    group_queries = lax.dynamic_slice_in_dim(
        queries, kv_head * group_size * head_width, group_size * head_width, 1
    )
    all_queries = lax.all_gather(group_queries, "dp", axis=0, tiled=True).reshape(
        requests, group_size, head_width
    )
    slot_branch = jnp.sum(
        jnp.where(
            slot_request[:, None] == jnp.arange(requests)[None, :], request_branch[None, :], 0
        ),
        axis=1,
    )
    slot_root = jnp.sum(
        jnp.where(
            slot_branch[:, None] == jnp.arange(branches)[None, :], branch_parent[None, :], 0
        ),
        axis=1,
    )
    local_roots = jnp.nonzero(root_owner == dp_index, size=ROOT_DEV)[0]
    local_branches = jnp.nonzero(branch_owner == dp_index, size=BR_DEV)[0]
    page_pool = node_cache[:, :, 0]
    flat_queries = all_queries.reshape(requests, group_size * head_width)

    def selection(node_of_slot, nodes, cap):
        hit = node_of_slot[None, :] == nodes[:, None]
        rank = jnp.cumsum(hit.astype(jnp.int32), axis=1) - 1
        return hit[:, None, :] & (rank[:, None, :] == jnp.arange(cap)[None, :, None])

    def level_rows(nodes, node_pages, node_len, cap):
        pick = selection(node_of_slot_for[cap], nodes, cap)
        member_queries = jnp.einsum(
            "nks,sx->nkx", pick.astype(jnp.bfloat16), flat_queries,
            preferred_element_type=jnp.float32,
        ).astype(jnp.bfloat16).reshape(nodes.shape[0], cap, group_size, head_width)
        page_list = jnp.take(node_pages, nodes, axis=0)
        blocks = jnp.take(page_pool, page_list.reshape(-1), axis=1).reshape(
            (2,) + page_list.shape + page_pool.shape[2:]
        )
        lengths = jnp.take(node_len, nodes)

        def one_node(queries_of, keys_of, values_of, length):
            page_count = keys_of.shape[0]
            positions = (
                jnp.arange(page_count)[:, None] * PAGE
                + part_index * token_width
                + jnp.arange(token_width)[None, :]
            ).reshape(-1)
            usable = (positions < length)[None, None, :]
            scores = jnp.einsum(
                "sgd,ld->sgl", queries_of, keys_of.reshape(-1, head_width),
                preferred_element_type=jnp.float32,
            ) * head_width ** (-0.5)
            return weigh_scores(scores, usable, values_of.reshape(-1, head_width), "sgl,ld->sgd")

        weighted_sum, row_max, weight_total = jax.vmap(one_node)(
            member_queries, blocks[0], blocks[1], lengths
        )
        stats = jnp.concatenate([row_max, weight_total], axis=2)
        stats = jnp.pad(stats, ((0, 0), (0, 0), (0, head_width - 2 * group_size)))
        rows = jnp.concatenate(
            [weighted_sum.reshape(nodes.shape[0], cap, group_size * head_width), stats], axis=2
        )
        return jnp.einsum(
            "nks,nkc->sc", pick.astype(jnp.float32), rows,
            precision=lax.Precision.HIGHEST, preferred_element_type=jnp.float32,
        )

    root_cap = (branches // root_count) * BR_CAP
    node_of_slot_for = {root_cap: slot_root, BR_CAP: slot_branch}
    root_rows = level_rows(local_roots, root_pages, root_len, root_cap)
    branch_rows = level_rows(local_branches, branch_pages, branch_len, BR_CAP)
    groups = group_size
    dp_count = lax.axis_size("dp")
    packed = jnp.concatenate([root_rows, branch_rows], axis=1)
    exchanged = lax.all_to_all(
        packed.reshape(dp_count, local_rows, (2 * groups + 2) * head_width),
        "dp",
        split_axis=0,
        concat_axis=0,
        tiled=True,
    )
    gathered = jnp.sum(exchanged, axis=0).reshape(local_rows, 2 * groups + 2, head_width)
    root_stats = gathered[:, groups]
    branch_stats = gathered[:, 2 * groups + 1]
    returned = (
        gathered[:, :groups],
        root_stats[:, :groups],
        root_stats[:, groups : 2 * groups],
        gathered[:, groups + 1 : 2 * groups + 1],
        branch_stats[:, :groups],
        branch_stats[:, groups : 2 * groups],
    )
    leaf_block = leaf_cache[:, :, 0]
    mine_queries = group_queries.reshape(local_rows, group_size, head_width)
    leaf_places = part_index * token_width + jnp.arange(token_width)
    leaf_usable = (leaf_places[None, :] < leaf_len[:, None])[:, None, :]
    leaf_scores = jnp.einsum(
        "rgd,rtd->rgt", mine_queries, leaf_block[0], preferred_element_type=jnp.float32
    ) * head_width ** (-0.5)
    leaf_partial = weigh_scores(leaf_scores, leaf_usable, leaf_block[1], "rgt,rtd->rgd")
    running = merge_partials(
        (returned[0], returned[1], returned[2]), (returned[3], returned[4], returned[5])
    )
    running = merge_partials(running, leaf_partial)
    bit_count = part_count.bit_length() - 1
    for bit_index in reversed(range(bit_count)):
        half_heads = running[1].shape[1] // 2
        upper_side = mp_index >> bit_index & 1 == 1
        kept_half = tuple(
            (
                jnp.where(upper_side, component[:, half_heads:], component[:, :half_heads])
                for component in running
            )
        )
        sent_half = tuple(
            (
                jnp.where(upper_side, component[:, :half_heads], component[:, half_heads:])
                for component in running
            )
        )
        received = partner((sent_half[0], sent_half[1], sent_half[2]), "mp", bit_index)
        running = merge_partials(kept_half, received)
    own_queries = lax.dynamic_slice_in_dim(
        queries, mp_index * own_heads * head_width, own_heads * head_width, 1
    ).reshape(local_rows, own_heads, head_width)
    fresh_kv = lax.dynamic_slice_in_dim(new_kv, kv_head * head_width, head_width, 2)
    self_score = jnp.einsum(
        "rhd,rd->rh", own_queries, fresh_kv[0], preferred_element_type=jnp.float32
    ) * head_width ** (-0.5)
    weighted, row_max, weight_total = running
    common_max = jnp.maximum(row_max, self_score)
    old_factor = jnp.exp(row_max - common_max)
    new_factor = jnp.exp(self_score - common_max)
    weighted = (
        weighted * old_factor[..., None]
        + new_factor[..., None] * fresh_kv[1].astype(jnp.float32)[:, None, :]
    )
    weight_total = weight_total * old_factor + new_factor
    attended = (
        (weighted / weight_total[..., None])
        .astype(jnp.bfloat16)
        .reshape(local_rows, own_heads * head_width)
    )
    projected = jnp.dot(attended, out_weight, preferred_element_type=jnp.float32)
    slice_width = residual.shape[1]
    mp_count = lax.axis_size("mp")
    start_col = mp_index * slice_width
    own_cols = lax.dynamic_slice_in_dim(projected, start_col, slice_width, 1) + residual.astype(
        jnp.float32
    )
    projected = lax.dynamic_update_slice_in_dim(projected, own_cols, start_col, 1)
    terms = projected.astype(jnp.bfloat16).reshape(local_rows, mp_count, slice_width)
    terms = jnp.transpose(terms, (1, 0, 2))
    received_terms = lax.all_to_all(terms, "mp", split_axis=0, concat_axis=0, tiled=True)
    kept_cols = jnp.sum(received_terms.astype(jnp.float32), axis=0)
    spread_cols = jnp.broadcast_to(
        kept_cols.astype(jnp.bfloat16)[None], (mp_count, local_rows, slice_width)
    )
    all_cols = lax.all_to_all(spread_cols, "mp", split_axis=0, concat_axis=0, tiled=True)
    hidden = jnp.transpose(all_cols, (1, 0, 2)).reshape(local_rows, -1).astype(jnp.float32)
    inv_rms = lax.rsqrt(jnp.mean(hidden * hidden, axis=1) + NORM_EPS)
    normed = (hidden * inv_rms[:, None] * norm_gain[None, :]).astype(jnp.bfloat16)
    logits = jnp.dot(normed, router, preferred_element_type=jnp.float32)
    route_hits = routes[:, :, None] == jnp.arange(EXPERTS)[None, None, :]
    chosen = jnp.sum(jnp.where(route_hits, logits[:, None, :], 0.0), axis=2)
    gate_weights = jax.nn.softmax(chosen, axis=1)
    pair_experts = routes.reshape(-1)
    pair_onehot = (pair_experts[:, None] == jnp.arange(EXPERTS)[None, :]).astype(jnp.int32)
    pair_rank = jnp.sum((jnp.cumsum(pair_onehot, axis=0) - 1) * pair_onehot, axis=1)
    pair_slot = pair_experts * E_CAP + pair_rank
    slot_source = (
        jnp.full((EXPERTS * E_CAP,), local_rows, jnp.int32)
        .at[pair_slot]
        .set(jnp.arange(pair_experts.shape[0], dtype=jnp.int32) // TOP)
    )
    padded = jnp.concatenate([normed, jnp.zeros((1, normed.shape[1]), jnp.bfloat16)], axis=0)
    local_experts = expert_in.shape[0]
    outgoing = jnp.take(padded, slot_source, axis=0).reshape(
        dp_count, local_experts, E_CAP, normed.shape[1]
    )
    returned_parts = []
    for expert_index in range(local_experts):
        incoming = lax.all_to_all(
            outgoing[:, expert_index], "dp", split_axis=0, concat_axis=0, tiled=True
        )
        gate_up = jnp.einsum(
            "scd,kfd->kscf", incoming, expert_in[expert_index], preferred_element_type=jnp.float32
        )
        expert_hidden = (jax.nn.silu(gate_up[0]) * gate_up[1]).astype(jnp.bfloat16)
        if expert_index == local_experts - 1 and local_experts > 1:
            pieces = jnp.einsum(
                "scf,fmd->mscd", expert_hidden,
                expert_out[expert_index].reshape(-1, mp_count, slice_width),
                preferred_element_type=jnp.float32,
            ).astype(jnp.bfloat16)
            gathered_pieces = lax.all_to_all(pieces, "mp", split_axis=0, concat_axis=0, tiled=True)
            summed = jnp.sum(gathered_pieces.astype(jnp.float32), axis=0).astype(jnp.bfloat16)
        else:
            expert_partial = jnp.einsum(
                "scf,fd->scd", expert_hidden, expert_out[expert_index],
                preferred_element_type=jnp.float32,
            )
            summed = lax.psum_scatter(
                expert_partial.astype(jnp.bfloat16), "mp", scatter_dimension=2, tiled=True
            )
        returned_parts.append(
            lax.all_to_all(summed, "dp", split_axis=0, concat_axis=0, tiled=True)
        )
    returned_rows = jnp.stack(returned_parts, axis=1)
    results = jnp.take(returned_rows.reshape(-1, slice_width), pair_slot, axis=0).reshape(
        local_rows, TOP, slice_width
    )
    layer_out = kept_cols + jnp.sum(gate_weights[:, :, None] * results.astype(jnp.float32), axis=1)
    return layer_out.astype(jnp.bfloat16)


def solution(mesh):
    placed = (
        P("dp", None),
        P(None, "dp", None),
        P("dp", "mp"),
        P("mp", None),
        P(),
        P(),
        P("dp", None, "mp", None),
        P("dp", "mp", None),
        P(None, "dp", "mp", None, None),
        P(None, "dp", "mp", None, None),
        P(),
        P(),
        P(),
        P(),
        P(),
        P(),
        P(),
        P(),
        P(),
        P("dp"),
        P("dp", None),
    )
    return jax.shard_map(
        shards, mesh=mesh, in_specs=placed, out_specs=P("dp", "mp"), check_vma=False
    )
```

```python
import jax
import jax.numpy as jnp
from jax import lax
from jax.sharding import PartitionSpec as P

HEADS = 32
KVH = 8
EXPERTS = 8
TOP = 2
PAGE = 128
ROOT_DEV = 2
BR_DEV = 8
BR_CAP = 32
E_CAP = 64


MASKED_SCORE = -1e30
NORM_EPS = 1e-05


def partner(x, axis, apart):
    return lax.ppermute(x, axis, [(i, i ^ 1 << apart) for i in range(lax.axis_size(axis))])


def merge_partials(first_part, second_part):
    first_sum, first_max, first_total = first_part
    second_sum, second_max, second_total = second_part
    common_max = jnp.maximum(first_max, second_max)
    first_factor = jnp.exp(first_max - common_max)
    second_factor = jnp.exp(second_max - common_max)
    merged_sum = first_sum * first_factor[..., None] + second_sum * second_factor[..., None]
    return (merged_sum, common_max, first_total * first_factor + second_total * second_factor)


def weigh_scores(scores, usable, values, pattern):
    masked_scores = jnp.where(usable, scores, MASKED_SCORE)
    row_max = jnp.max(masked_scores, axis=-1)
    weights = jnp.where(usable, jnp.exp(masked_scores - row_max[..., None]), 0.0)
    weight_total = jnp.sum(weights, axis=-1)
    weighted_sum = jnp.einsum(
        pattern, weights.astype(jnp.bfloat16), values, preferred_element_type=jnp.float32
    )
    return (weighted_sum, row_max, weight_total)


def shards(
    queries,
    new_kv,
    residual,
    out_weight,
    norm_gain,
    router,
    expert_in,
    expert_out,
    node_cache,
    leaf_cache,
    slot_request,
    request_branch,
    branch_parent,
    root_owner,
    branch_owner,
    root_pages,
    branch_pages,
    root_len,
    branch_len,
    leaf_len,
    routes,
):
    head_width = node_cache.shape[-1]
    token_width = node_cache.shape[-2]
    part_count = lax.axis_size("mp") // KVH
    group_size = HEADS // KVH
    own_heads = HEADS // lax.axis_size("mp")
    local_rows = queries.shape[0]
    requests = slot_request.shape[0]
    branches = branch_parent.shape[0]
    root_count = root_owner.shape[0]
    mp_index = lax.axis_index("mp")
    dp_index = lax.axis_index("dp")
    kv_head = mp_index // part_count
    part_index = mp_index % part_count
    group_queries = lax.dynamic_slice_in_dim(
        queries, kv_head * group_size * head_width, group_size * head_width, 1
    )
    all_queries = lax.all_gather(group_queries, "dp", axis=0, tiled=True).reshape(
        requests, group_size, head_width
    )
    slot_branch = jnp.sum(
        jnp.where(
            slot_request[:, None] == jnp.arange(requests)[None, :], request_branch[None, :], 0
        ),
        axis=1,
    )
    slot_root = jnp.sum(
        jnp.where(
            slot_branch[:, None] == jnp.arange(branches)[None, :], branch_parent[None, :], 0
        ),
        axis=1,
    )
    local_roots = jnp.nonzero(root_owner == dp_index, size=ROOT_DEV)[0]
    local_branches = jnp.nonzero(branch_owner == dp_index, size=BR_DEV)[0]
    page_pool = node_cache[:, :, 0]
    flat_queries = all_queries.reshape(requests, group_size * head_width)

    def selection(node_of_slot, nodes, cap):
        hit = node_of_slot[None, :] == nodes[:, None]
        rank = jnp.cumsum(hit.astype(jnp.int32), axis=1) - 1
        return hit[:, None, :] & (rank[:, None, :] == jnp.arange(cap)[None, :, None])

    def level_rows(nodes, node_pages, node_len, cap):
        pick = selection(node_of_slot_for[cap], nodes, cap)
        member_queries = jnp.einsum(
            "nks,sx->nkx", pick.astype(jnp.bfloat16), flat_queries,
            preferred_element_type=jnp.float32,
        ).astype(jnp.bfloat16).reshape(nodes.shape[0], cap, group_size, head_width)
        page_list = jnp.take(node_pages, nodes, axis=0)
        blocks = jnp.take(page_pool, page_list.reshape(-1), axis=1).reshape(
            (2,) + page_list.shape + page_pool.shape[2:]
        )
        lengths = jnp.take(node_len, nodes)

        def one_node(queries_of, keys_of, values_of, length):
            page_count = keys_of.shape[0]
            positions = (
                jnp.arange(page_count)[:, None] * PAGE
                + part_index * token_width
                + jnp.arange(token_width)[None, :]
            ).reshape(-1)
            usable = (positions < length)[None, None, :]
            scores = jnp.einsum(
                "sgd,ld->sgl", queries_of, keys_of.reshape(-1, head_width),
                preferred_element_type=jnp.float32,
            ) * head_width ** (-0.5)
            return weigh_scores(scores, usable, values_of.reshape(-1, head_width), "sgl,ld->sgd")

        weighted_sum, row_max, weight_total = jax.vmap(one_node)(
            member_queries, blocks[0], blocks[1], lengths
        )
        stats = jnp.concatenate([row_max, weight_total], axis=2)
        stats = jnp.pad(stats, ((0, 0), (0, 0), (0, head_width - 2 * group_size)))
        rows = jnp.concatenate(
            [weighted_sum.reshape(nodes.shape[0], cap, group_size * head_width), stats], axis=2
        )
        return jnp.einsum(
            "nks,nkc->sc", pick.astype(jnp.float32), rows,
            precision=lax.Precision.HIGHEST, preferred_element_type=jnp.float32,
        )

    root_cap = (branches // root_count) * BR_CAP
    node_of_slot_for = {root_cap: slot_root, BR_CAP: slot_branch}
    root_rows = level_rows(local_roots, root_pages, root_len, root_cap)
    branch_rows = level_rows(local_branches, branch_pages, branch_len, BR_CAP)
    groups = group_size
    dp_count = lax.axis_size("dp")
    packed = jnp.concatenate([root_rows, branch_rows], axis=1)
    exchanged = lax.all_to_all(
        packed.reshape(dp_count, local_rows, (2 * groups + 2) * head_width),
        "dp",
        split_axis=0,
        concat_axis=0,
        tiled=True,
    )
    gathered = jnp.sum(exchanged, axis=0).reshape(local_rows, 2 * groups + 2, head_width)
    root_stats = gathered[:, groups]
    branch_stats = gathered[:, 2 * groups + 1]
    returned = (
        gathered[:, :groups],
        root_stats[:, :groups],
        root_stats[:, groups : 2 * groups],
        gathered[:, groups + 1 : 2 * groups + 1],
        branch_stats[:, :groups],
        branch_stats[:, groups : 2 * groups],
    )
    leaf_block = leaf_cache[:, :, 0]
    mine_queries = group_queries.reshape(local_rows, group_size, head_width)
    leaf_places = part_index * token_width + jnp.arange(token_width)
    leaf_usable = (leaf_places[None, :] < leaf_len[:, None])[:, None, :]
    leaf_scores = jnp.einsum(
        "rgd,rtd->rgt", mine_queries, leaf_block[0], preferred_element_type=jnp.float32
    ) * head_width ** (-0.5)
    leaf_partial = weigh_scores(leaf_scores, leaf_usable, leaf_block[1], "rgt,rtd->rgd")
    running = merge_partials(
        (returned[0], returned[1], returned[2]), (returned[3], returned[4], returned[5])
    )
    running = merge_partials(running, leaf_partial)
    bit_count = part_count.bit_length() - 1
    for bit_index in reversed(range(bit_count)):
        half_heads = running[1].shape[1] // 2
        upper_side = mp_index >> bit_index & 1 == 1
        kept_half = tuple(
            (
                jnp.where(upper_side, component[:, half_heads:], component[:, :half_heads])
                for component in running
            )
        )
        sent_half = tuple(
            (
                jnp.where(upper_side, component[:, :half_heads], component[:, half_heads:])
                for component in running
            )
        )
        received = partner((sent_half[0], sent_half[1], sent_half[2]), "mp", bit_index)
        running = merge_partials(kept_half, received)
    own_queries = lax.dynamic_slice_in_dim(
        queries, mp_index * own_heads * head_width, own_heads * head_width, 1
    ).reshape(local_rows, own_heads, head_width)
    fresh_kv = lax.dynamic_slice_in_dim(new_kv, kv_head * head_width, head_width, 2)
    self_score = jnp.einsum(
        "rhd,rd->rh", own_queries, fresh_kv[0], preferred_element_type=jnp.float32
    ) * head_width ** (-0.5)
    weighted, row_max, weight_total = running
    common_max = jnp.maximum(row_max, self_score)
    old_factor = jnp.exp(row_max - common_max)
    new_factor = jnp.exp(self_score - common_max)
    weighted = (
        weighted * old_factor[..., None]
        + new_factor[..., None] * fresh_kv[1].astype(jnp.float32)[:, None, :]
    )
    weight_total = weight_total * old_factor + new_factor
    attended = (
        (weighted / weight_total[..., None])
        .astype(jnp.bfloat16)
        .reshape(local_rows, own_heads * head_width)
    )
    projected = jnp.dot(attended, out_weight, preferred_element_type=jnp.float32)
    slice_width = residual.shape[1]
    mp_count = lax.axis_size("mp")
    start_col = mp_index * slice_width
    own_cols = lax.dynamic_slice_in_dim(projected, start_col, slice_width, 1) + residual.astype(
        jnp.float32
    )
    projected = lax.dynamic_update_slice_in_dim(projected, own_cols, start_col, 1)
    terms = projected.astype(jnp.bfloat16).reshape(local_rows, mp_count, slice_width)
    terms = jnp.transpose(terms, (1, 0, 2))
    received_terms = lax.all_to_all(terms, "mp", split_axis=0, concat_axis=0, tiled=True)
    kept_cols = jnp.sum(received_terms.astype(jnp.float32), axis=0)
    spread_cols = jnp.broadcast_to(
        kept_cols.astype(jnp.bfloat16)[None], (mp_count, local_rows, slice_width)
    )
    all_cols = lax.all_to_all(spread_cols, "mp", split_axis=0, concat_axis=0, tiled=True)
    hidden = jnp.transpose(all_cols, (1, 0, 2)).reshape(local_rows, -1).astype(jnp.float32)
    inv_rms = lax.rsqrt(jnp.mean(hidden * hidden, axis=1) + NORM_EPS)
    normed = (hidden * inv_rms[:, None] * norm_gain[None, :]).astype(jnp.bfloat16)
    logits = jnp.dot(normed, router, preferred_element_type=jnp.float32)
    route_hits = routes[:, :, None] == jnp.arange(EXPERTS)[None, None, :]
    chosen = jnp.sum(jnp.where(route_hits, logits[:, None, :], 0.0), axis=2)
    gate_weights = jax.nn.softmax(chosen, axis=1)
    pair_experts = routes.reshape(-1)
    pair_onehot = (pair_experts[:, None] == jnp.arange(EXPERTS)[None, :]).astype(jnp.int32)
    pair_rank = jnp.sum((jnp.cumsum(pair_onehot, axis=0) - 1) * pair_onehot, axis=1)
    pair_slot = pair_experts * E_CAP + pair_rank
    slot_source = (
        jnp.full((EXPERTS * E_CAP,), local_rows, jnp.int32)
        .at[pair_slot]
        .set(jnp.arange(pair_experts.shape[0], dtype=jnp.int32) // TOP)
    )
    padded = jnp.concatenate([normed, jnp.zeros((1, normed.shape[1]), jnp.bfloat16)], axis=0)
    local_experts = expert_in.shape[0]
    outgoing = jnp.take(padded, slot_source, axis=0).reshape(
        dp_count, local_experts, E_CAP, normed.shape[1]
    )
    returned_parts = []
    for expert_index in range(local_experts):
        incoming = lax.all_to_all(
            outgoing[:, expert_index], "dp", split_axis=0, concat_axis=0, tiled=True
        )
        by_mesh = expert_index == local_experts - 1 and local_experts > 1 and dp_count % 2 == 0
        halves = 2 if by_mesh else 1
        pieces_summed = []
        for half in range(halves):
            sources = dp_count // halves
            chunk = incoming[half * sources : (half + 1) * sources]
            gate_up = jnp.einsum(
                "scd,kfd->kscf", chunk, expert_in[expert_index], preferred_element_type=jnp.float32
            )
            expert_hidden = (jax.nn.silu(gate_up[0]) * gate_up[1]).astype(jnp.bfloat16)
            expert_partial = jnp.einsum(
                "scf,fd->scd", expert_hidden, expert_out[expert_index],
                preferred_element_type=jnp.float32,
            ).astype(jnp.bfloat16)
            if by_mesh:
                pieces = expert_partial.reshape(sources, E_CAP, mp_count, slice_width)
                gathered_pieces = lax.all_to_all(
                    pieces, "mp", split_axis=2, concat_axis=2, tiled=True
                )
                pieces_summed.append(
                    jnp.sum(gathered_pieces.astype(jnp.float32), axis=2).astype(jnp.bfloat16)
                )
            else:
                pieces_summed.append(
                    lax.psum_scatter(expert_partial, "mp", scatter_dimension=2, tiled=True)
                )
        summed = jnp.concatenate(pieces_summed, axis=0)
        returned_parts.append(
            lax.all_to_all(summed, "dp", split_axis=0, concat_axis=0, tiled=True)
        )
    returned_rows = jnp.stack(returned_parts, axis=1)
    results = jnp.take(returned_rows.reshape(-1, slice_width), pair_slot, axis=0).reshape(
        local_rows, TOP, slice_width
    )
    layer_out = kept_cols + jnp.sum(gate_weights[:, :, None] * results.astype(jnp.float32), axis=1)
    return layer_out.astype(jnp.bfloat16)


def solution(mesh):
    placed = (
        P("dp", None),
        P(None, "dp", None),
        P("dp", "mp"),
        P("mp", None),
        P(),
        P(),
        P("dp", None, "mp", None),
        P("dp", "mp", None),
        P(None, "dp", "mp", None, None),
        P(None, "dp", "mp", None, None),
        P(),
        P(),
        P(),
        P(),
        P(),
        P(),
        P(),
        P(),
        P(),
        P("dp"),
        P("dp", None),
    )
    return jax.shard_map(
        shards, mesh=mesh, in_specs=placed, out_specs=P("dp", "mp"), check_vma=False
    )
```

```python
import jax
import jax.numpy as jnp
from jax import lax
from jax.sharding import PartitionSpec as P

HEADS = 32
KVH = 8
EXPERTS = 8
TOP = 2
PAGE = 128
ROOT_DEV = 2
BR_DEV = 8
BR_CAP = 32
E_CAP = 64


MASKED_SCORE = -1e30
NORM_EPS = 1e-05


def partner(x, axis, apart):
    return lax.ppermute(x, axis, [(i, i ^ 1 << apart) for i in range(lax.axis_size(axis))])


def merge_partials(first_part, second_part):
    first_sum, first_max, first_total = first_part
    second_sum, second_max, second_total = second_part
    common_max = jnp.maximum(first_max, second_max)
    first_factor = jnp.exp(first_max - common_max)
    second_factor = jnp.exp(second_max - common_max)
    merged_sum = first_sum * first_factor[..., None] + second_sum * second_factor[..., None]
    return (merged_sum, common_max, first_total * first_factor + second_total * second_factor)


def weigh_scores(scores, usable, values, pattern):
    masked_scores = jnp.where(usable, scores, MASKED_SCORE)
    row_max = jnp.max(masked_scores, axis=-1)
    weights = jnp.where(usable, jnp.exp(masked_scores - row_max[..., None]), 0.0)
    weight_total = jnp.sum(weights, axis=-1)
    weighted_sum = jnp.einsum(
        pattern, weights.astype(jnp.bfloat16), values, preferred_element_type=jnp.float32
    )
    return (weighted_sum, row_max, weight_total)


def shards(
    queries,
    new_kv,
    residual,
    out_weight,
    norm_gain,
    router,
    expert_in,
    expert_out,
    node_cache,
    leaf_cache,
    slot_request,
    request_branch,
    branch_parent,
    root_owner,
    branch_owner,
    root_pages,
    branch_pages,
    root_len,
    branch_len,
    leaf_len,
    routes,
):
    head_width = node_cache.shape[-1]
    token_width = node_cache.shape[-2]
    part_count = lax.axis_size("mp") // KVH
    group_size = HEADS // KVH
    own_heads = HEADS // lax.axis_size("mp")
    local_rows = queries.shape[0]
    requests = slot_request.shape[0]
    branches = branch_parent.shape[0]
    root_count = root_owner.shape[0]
    mp_index = lax.axis_index("mp")
    dp_index = lax.axis_index("dp")
    kv_head = mp_index // part_count
    part_index = mp_index % part_count
    group_queries = lax.dynamic_slice_in_dim(
        queries, kv_head * group_size * head_width, group_size * head_width, 1
    )
    all_queries = lax.all_gather(group_queries, "dp", axis=0, tiled=True).reshape(
        requests, group_size, head_width
    )
    slot_branch = jnp.sum(
        jnp.where(
            slot_request[:, None] == jnp.arange(requests)[None, :], request_branch[None, :], 0
        ),
        axis=1,
    )
    slot_root = jnp.sum(
        jnp.where(
            slot_branch[:, None] == jnp.arange(branches)[None, :], branch_parent[None, :], 0
        ),
        axis=1,
    )
    local_roots = jnp.nonzero(root_owner == dp_index, size=ROOT_DEV)[0]
    local_branches = jnp.nonzero(branch_owner == dp_index, size=BR_DEV)[0]
    page_pool = node_cache[:, :, 0]
    flat_queries = all_queries.reshape(requests, group_size * head_width)

    def selection(node_of_slot, nodes, cap):
        hit = node_of_slot[None, :] == nodes[:, None]
        rank = jnp.cumsum(hit.astype(jnp.int32), axis=1) - 1
        return hit[:, None, :] & (rank[:, None, :] == jnp.arange(cap)[None, :, None])

    def level_rows(nodes, node_pages, node_len, cap):
        pick = selection(node_of_slot_for[cap], nodes, cap)
        member_queries = jnp.einsum(
            "nks,sx->nkx", pick.astype(jnp.bfloat16), flat_queries,
            preferred_element_type=jnp.float32,
        ).astype(jnp.bfloat16).reshape(nodes.shape[0], cap, group_size, head_width)
        page_list = jnp.take(node_pages, nodes, axis=0)
        blocks = jnp.take(page_pool, page_list.reshape(-1), axis=1).reshape(
            (2,) + page_list.shape + page_pool.shape[2:]
        )
        lengths = jnp.take(node_len, nodes)

        def one_node(queries_of, keys_of, values_of, length):
            page_count = keys_of.shape[0]
            positions = (
                jnp.arange(page_count)[:, None] * PAGE
                + part_index * token_width
                + jnp.arange(token_width)[None, :]
            ).reshape(-1)
            usable = (positions < length)[None, None, :]
            scores = jnp.einsum(
                "sgd,ld->sgl", queries_of, keys_of.reshape(-1, head_width),
                preferred_element_type=jnp.float32,
            ) * head_width ** (-0.5)
            return weigh_scores(scores, usable, values_of.reshape(-1, head_width), "sgl,ld->sgd")

        weighted_sum, row_max, weight_total = jax.vmap(one_node)(
            member_queries, blocks[0], blocks[1], lengths
        )
        stats = jnp.concatenate([row_max, weight_total], axis=2)
        stats = jnp.pad(stats, ((0, 0), (0, 0), (0, head_width - 2 * group_size)))
        rows = jnp.concatenate(
            [weighted_sum.reshape(nodes.shape[0], cap, group_size * head_width), stats], axis=2
        )
        return jnp.einsum(
            "nks,nkc->sc", pick.astype(jnp.float32), rows,
            precision=lax.Precision.HIGHEST, preferred_element_type=jnp.float32,
        )

    root_cap = (branches // root_count) * BR_CAP
    node_of_slot_for = {root_cap: slot_root, BR_CAP: slot_branch}
    root_rows = level_rows(local_roots, root_pages, root_len, root_cap)
    branch_rows = level_rows(local_branches, branch_pages, branch_len, BR_CAP)
    groups = group_size
    dp_count = lax.axis_size("dp")
    stats = jnp.concatenate(
        [root_rows[:, groups * head_width : (groups * head_width + 2 * groups)],
         branch_rows[:, groups * head_width : (groups * head_width + 2 * groups)]],
        axis=1,
    )
    stats_high = lax.reduce_precision(stats, exponent_bits=8, mantissa_bits=7)
    stats_rest = stats - stats_high
    stats_mid = lax.reduce_precision(stats_rest, exponent_bits=8, mantissa_bits=7)
    stats_low = stats_rest - stats_mid
    stat_block = jnp.concatenate([stats_high, stats_mid, stats_low], axis=1).astype(jnp.bfloat16)
    stat_block = jnp.pad(stat_block, ((0, 0), (0, head_width - stat_block.shape[1])))
    packed = jnp.concatenate(
        [root_rows[:, : groups * head_width].astype(jnp.bfloat16),
         branch_rows[:, : groups * head_width].astype(jnp.bfloat16),
         stat_block],
        axis=1,
    )
    exchanged = lax.all_to_all(
        packed.reshape(dp_count, local_rows, packed.shape[1]),
        "dp",
        split_axis=0,
        concat_axis=0,
        tiled=True,
    )
    gathered = jnp.sum(exchanged.astype(jnp.float32), axis=0)
    sum_width = groups * head_width
    stat_width = 4 * groups
    stat_parts = gathered[:, 2 * sum_width :]
    joined = (
        stat_parts[:, :stat_width] + stat_parts[:, stat_width : 2 * stat_width]
    ) + stat_parts[:, 2 * stat_width : 3 * stat_width]
    returned = (
        gathered[:, :sum_width].reshape(local_rows, groups, head_width),
        joined[:, :groups],
        joined[:, groups : 2 * groups],
        gathered[:, sum_width : 2 * sum_width].reshape(local_rows, groups, head_width),
        joined[:, 2 * groups : 3 * groups],
        joined[:, 3 * groups : 4 * groups],
    )
    leaf_block = leaf_cache[:, :, 0]
    mine_queries = group_queries.reshape(local_rows, group_size, head_width)
    leaf_places = part_index * token_width + jnp.arange(token_width)
    leaf_usable = (leaf_places[None, :] < leaf_len[:, None])[:, None, :]
    leaf_scores = jnp.einsum(
        "rgd,rtd->rgt", mine_queries, leaf_block[0], preferred_element_type=jnp.float32
    ) * head_width ** (-0.5)
    leaf_partial = weigh_scores(leaf_scores, leaf_usable, leaf_block[1], "rgt,rtd->rgd")
    running = merge_partials(
        (returned[0], returned[1], returned[2]), (returned[3], returned[4], returned[5])
    )
    running = merge_partials(running, leaf_partial)
    bit_count = part_count.bit_length() - 1
    for bit_index in reversed(range(bit_count)):
        half_heads = running[1].shape[1] // 2
        upper_side = mp_index >> bit_index & 1 == 1
        kept_half = tuple(
            (
                jnp.where(upper_side, component[:, half_heads:], component[:, :half_heads])
                for component in running
            )
        )
        sent_half = tuple(
            (
                jnp.where(upper_side, component[:, :half_heads], component[:, half_heads:])
                for component in running
            )
        )
        received = partner((sent_half[0], sent_half[1], sent_half[2]), "mp", bit_index)
        running = merge_partials(kept_half, received)
    own_queries = lax.dynamic_slice_in_dim(
        queries, mp_index * own_heads * head_width, own_heads * head_width, 1
    ).reshape(local_rows, own_heads, head_width)
    fresh_kv = lax.dynamic_slice_in_dim(new_kv, kv_head * head_width, head_width, 2)
    self_score = jnp.einsum(
        "rhd,rd->rh", own_queries, fresh_kv[0], preferred_element_type=jnp.float32
    ) * head_width ** (-0.5)
    weighted, row_max, weight_total = running
    common_max = jnp.maximum(row_max, self_score)
    old_factor = jnp.exp(row_max - common_max)
    new_factor = jnp.exp(self_score - common_max)
    weighted = (
        weighted * old_factor[..., None]
        + new_factor[..., None] * fresh_kv[1].astype(jnp.float32)[:, None, :]
    )
    weight_total = weight_total * old_factor + new_factor
    attended = (
        (weighted / weight_total[..., None])
        .astype(jnp.bfloat16)
        .reshape(local_rows, own_heads * head_width)
    )
    projected = jnp.dot(attended, out_weight, preferred_element_type=jnp.float32)
    slice_width = residual.shape[1]
    mp_count = lax.axis_size("mp")
    start_col = mp_index * slice_width
    own_cols = lax.dynamic_slice_in_dim(projected, start_col, slice_width, 1) + residual.astype(
        jnp.float32
    )
    projected = lax.dynamic_update_slice_in_dim(projected, own_cols, start_col, 1)
    terms = projected.astype(jnp.bfloat16).reshape(local_rows, mp_count, slice_width)
    terms = jnp.transpose(terms, (1, 0, 2))
    received_terms = lax.all_to_all(terms, "mp", split_axis=0, concat_axis=0, tiled=True)
    kept_cols = jnp.sum(received_terms.astype(jnp.float32), axis=0)
    spread_cols = jnp.broadcast_to(
        kept_cols.astype(jnp.bfloat16)[None], (mp_count, local_rows, slice_width)
    )
    all_cols = lax.all_to_all(spread_cols, "mp", split_axis=0, concat_axis=0, tiled=True)
    hidden = jnp.transpose(all_cols, (1, 0, 2)).reshape(local_rows, -1).astype(jnp.float32)
    inv_rms = lax.rsqrt(jnp.mean(hidden * hidden, axis=1) + NORM_EPS)
    normed = (hidden * inv_rms[:, None] * norm_gain[None, :]).astype(jnp.bfloat16)
    logits = jnp.dot(normed, router, preferred_element_type=jnp.float32)
    route_hits = routes[:, :, None] == jnp.arange(EXPERTS)[None, None, :]
    chosen = jnp.sum(jnp.where(route_hits, logits[:, None, :], 0.0), axis=2)
    gate_weights = jax.nn.softmax(chosen, axis=1)
    pair_experts = routes.reshape(-1)
    pair_onehot = (pair_experts[:, None] == jnp.arange(EXPERTS)[None, :]).astype(jnp.int32)
    pair_rank = jnp.sum((jnp.cumsum(pair_onehot, axis=0) - 1) * pair_onehot, axis=1)
    pair_slot = pair_experts * E_CAP + pair_rank
    slot_source = (
        jnp.full((EXPERTS * E_CAP,), local_rows, jnp.int32)
        .at[pair_slot]
        .set(jnp.arange(pair_experts.shape[0], dtype=jnp.int32) // TOP)
    )
    padded = jnp.concatenate([normed, jnp.zeros((1, normed.shape[1]), jnp.bfloat16)], axis=0)
    local_experts = expert_in.shape[0]
    outgoing = jnp.take(padded, slot_source, axis=0).reshape(
        dp_count, local_experts, E_CAP, normed.shape[1]
    )
    returned_parts = []
    for expert_index in range(local_experts):
        incoming = lax.all_to_all(
            outgoing[:, expert_index], "dp", split_axis=0, concat_axis=0, tiled=True
        )
        gate_up = jnp.einsum(
            "scd,kfd->kscf", incoming, expert_in[expert_index], preferred_element_type=jnp.float32
        )
        expert_hidden = (jax.nn.silu(gate_up[0]) * gate_up[1]).astype(jnp.bfloat16)
        if expert_index == local_experts - 1 and local_experts > 1:
            pieces = jnp.einsum(
                "scf,fmd->mscd", expert_hidden,
                expert_out[expert_index].reshape(-1, mp_count, slice_width),
                preferred_element_type=jnp.float32,
            ).astype(jnp.bfloat16)
            gathered_pieces = lax.all_to_all(pieces, "mp", split_axis=0, concat_axis=0, tiled=True)
            summed = jnp.sum(gathered_pieces.astype(jnp.float32), axis=0).astype(jnp.bfloat16)
        else:
            expert_partial = jnp.einsum(
                "scf,fd->scd", expert_hidden, expert_out[expert_index],
                preferred_element_type=jnp.float32,
            )
            summed = lax.psum_scatter(
                expert_partial.astype(jnp.bfloat16), "mp", scatter_dimension=2, tiled=True
            )
        returned_parts.append(
            lax.all_to_all(summed, "dp", split_axis=0, concat_axis=0, tiled=True)
        )
    returned_rows = jnp.stack(returned_parts, axis=1)
    results = jnp.take(returned_rows.reshape(-1, slice_width), pair_slot, axis=0).reshape(
        local_rows, TOP, slice_width
    )
    layer_out = kept_cols + jnp.sum(gate_weights[:, :, None] * results.astype(jnp.float32), axis=1)
    return layer_out.astype(jnp.bfloat16)


def solution(mesh):
    placed = (
        P("dp", None),
        P(None, "dp", None),
        P("dp", "mp"),
        P("mp", None),
        P(),
        P(),
        P("dp", None, "mp", None),
        P("dp", "mp", None),
        P(None, "dp", "mp", None, None),
        P(None, "dp", "mp", None, None),
        P(),
        P(),
        P(),
        P(),
        P(),
        P(),
        P(),
        P(),
        P(),
        P("dp"),
        P("dp", None),
    )
    return jax.shard_map(
        shards, mesh=mesh, in_specs=placed, out_specs=P("dp", "mp"), check_vma=False
    )
```

```python
import jax
import jax.numpy as jnp
from jax import lax
from jax.sharding import PartitionSpec as P

HEADS = 32
KVH = 8
EXPERTS = 8
TOP = 2
PAGE = 128
ROOT_DEV = 2
BR_DEV = 8
BR_CAP = 32
E_CAP = 64


MASKED_SCORE = -1e30
NORM_EPS = 1e-05


def partner(x, axis, apart):
    return lax.ppermute(x, axis, [(i, i ^ 1 << apart) for i in range(lax.axis_size(axis))])


def merge_partials(first_part, second_part):
    first_sum, first_max, first_total = first_part
    second_sum, second_max, second_total = second_part
    common_max = jnp.maximum(first_max, second_max)
    first_factor = jnp.exp(first_max - common_max)
    second_factor = jnp.exp(second_max - common_max)
    merged_sum = first_sum * first_factor[..., None] + second_sum * second_factor[..., None]
    return (merged_sum, common_max, first_total * first_factor + second_total * second_factor)


def weigh_scores(scores, usable, values, pattern):
    masked_scores = jnp.where(usable, scores, MASKED_SCORE)
    row_max = jnp.max(masked_scores, axis=-1)
    weights = jnp.where(usable, jnp.exp(masked_scores - row_max[..., None]), 0.0)
    weight_total = jnp.sum(weights, axis=-1)
    weighted_sum = jnp.einsum(
        pattern, weights.astype(jnp.bfloat16), values, preferred_element_type=jnp.float32
    )
    return (weighted_sum, row_max, weight_total)


def halving_scatter(held, axis, block_axis):
    size = lax.axis_size(axis)
    me = lax.axis_index(axis)
    for bit in range(size.bit_length() - 1):
        shape = held.shape
        split = shape[:block_axis] + (shape[block_axis] // 2, 2) + shape[block_axis + 1 :]
        pairs = held.reshape(split)
        even = lax.index_in_dim(pairs, 0, block_axis + 1, keepdims=False)
        odd = lax.index_in_dim(pairs, 1, block_axis + 1, keepdims=False)
        upper = (me >> bit) & 1 == 1
        kept = jnp.where(upper, odd, even)
        sent = jnp.where(upper, even, odd).astype(jnp.bfloat16)
        received = lax.ppermute(sent, axis, [(i, i ^ (1 << bit)) for i in range(size)])
        held = kept + received.astype(jnp.float32)
    return lax.index_in_dim(held, 0, block_axis, keepdims=False)


def shards(
    queries,
    new_kv,
    residual,
    out_weight,
    norm_gain,
    router,
    expert_in,
    expert_out,
    node_cache,
    leaf_cache,
    slot_request,
    request_branch,
    branch_parent,
    root_owner,
    branch_owner,
    root_pages,
    branch_pages,
    root_len,
    branch_len,
    leaf_len,
    routes,
):
    head_width = node_cache.shape[-1]
    token_width = node_cache.shape[-2]
    part_count = lax.axis_size("mp") // KVH
    group_size = HEADS // KVH
    own_heads = HEADS // lax.axis_size("mp")
    local_rows = queries.shape[0]
    requests = slot_request.shape[0]
    branches = branch_parent.shape[0]
    root_count = root_owner.shape[0]
    mp_index = lax.axis_index("mp")
    dp_index = lax.axis_index("dp")
    kv_head = mp_index // part_count
    part_index = mp_index % part_count
    group_queries = lax.dynamic_slice_in_dim(
        queries, kv_head * group_size * head_width, group_size * head_width, 1
    )
    all_queries = lax.all_gather(group_queries, "dp", axis=0, tiled=True).reshape(
        requests, group_size, head_width
    )
    slot_branch = jnp.sum(
        jnp.where(
            slot_request[:, None] == jnp.arange(requests)[None, :], request_branch[None, :], 0
        ),
        axis=1,
    )
    slot_root = jnp.sum(
        jnp.where(
            slot_branch[:, None] == jnp.arange(branches)[None, :], branch_parent[None, :], 0
        ),
        axis=1,
    )
    local_roots = jnp.nonzero(root_owner == dp_index, size=ROOT_DEV)[0]
    local_branches = jnp.nonzero(branch_owner == dp_index, size=BR_DEV)[0]
    page_pool = node_cache[:, :, 0]
    flat_queries = all_queries.reshape(requests, group_size * head_width)

    def selection(node_of_slot, nodes, cap):
        hit = node_of_slot[None, :] == nodes[:, None]
        rank = jnp.cumsum(hit.astype(jnp.int32), axis=1) - 1
        return hit[:, None, :] & (rank[:, None, :] == jnp.arange(cap)[None, :, None])

    def level_rows(nodes, node_pages, node_len, cap):
        pick = selection(node_of_slot_for[cap], nodes, cap)
        member_queries = jnp.einsum(
            "nks,sx->nkx", pick.astype(jnp.bfloat16), flat_queries,
            preferred_element_type=jnp.float32,
        ).astype(jnp.bfloat16).reshape(nodes.shape[0], cap, group_size, head_width)
        page_list = jnp.take(node_pages, nodes, axis=0)
        blocks = jnp.take(page_pool, page_list.reshape(-1), axis=1).reshape(
            (2,) + page_list.shape + page_pool.shape[2:]
        )
        lengths = jnp.take(node_len, nodes)

        def one_node(queries_of, keys_of, values_of, length):
            page_count = keys_of.shape[0]
            positions = (
                jnp.arange(page_count)[:, None] * PAGE
                + part_index * token_width
                + jnp.arange(token_width)[None, :]
            ).reshape(-1)
            usable = (positions < length)[None, None, :]
            scores = jnp.einsum(
                "sgd,ld->sgl", queries_of, keys_of.reshape(-1, head_width),
                preferred_element_type=jnp.float32,
            ) * head_width ** (-0.5)
            return weigh_scores(scores, usable, values_of.reshape(-1, head_width), "sgl,ld->sgd")

        weighted_sum, row_max, weight_total = jax.vmap(one_node)(
            member_queries, blocks[0], blocks[1], lengths
        )
        stats = jnp.concatenate([row_max, weight_total], axis=2)
        stats = jnp.pad(stats, ((0, 0), (0, 0), (0, head_width - 2 * group_size)))
        rows = jnp.concatenate(
            [weighted_sum.reshape(nodes.shape[0], cap, group_size * head_width), stats], axis=2
        )
        return jnp.einsum(
            "nks,nkc->sc", pick.astype(jnp.float32), rows,
            precision=lax.Precision.HIGHEST, preferred_element_type=jnp.float32,
        )

    root_cap = (branches // root_count) * BR_CAP
    node_of_slot_for = {root_cap: slot_root, BR_CAP: slot_branch}
    root_rows = level_rows(local_roots, root_pages, root_len, root_cap)
    branch_rows = level_rows(local_branches, branch_pages, branch_len, BR_CAP)
    groups = group_size
    dp_count = lax.axis_size("dp")
    stats = jnp.concatenate(
        [root_rows[:, groups * head_width : (groups * head_width + 2 * groups)],
         branch_rows[:, groups * head_width : (groups * head_width + 2 * groups)]],
        axis=1,
    )
    stats_high = lax.reduce_precision(stats, exponent_bits=8, mantissa_bits=7)
    stats_rest = stats - stats_high
    stats_mid = lax.reduce_precision(stats_rest, exponent_bits=8, mantissa_bits=7)
    stats_low = stats_rest - stats_mid
    stat_block = jnp.concatenate([stats_high, stats_mid, stats_low], axis=1).astype(jnp.bfloat16)
    stat_block = jnp.pad(stat_block, ((0, 0), (0, head_width - stat_block.shape[1])))
    packed = jnp.concatenate(
        [root_rows[:, : groups * head_width].astype(jnp.bfloat16),
         branch_rows[:, : groups * head_width].astype(jnp.bfloat16),
         stat_block],
        axis=1,
    )
    exchanged = lax.all_to_all(
        packed.reshape(dp_count, local_rows, packed.shape[1]),
        "dp",
        split_axis=0,
        concat_axis=0,
        tiled=True,
    )
    gathered = jnp.sum(exchanged.astype(jnp.float32), axis=0)
    sum_width = groups * head_width
    stat_width = 4 * groups
    stat_parts = gathered[:, 2 * sum_width :]
    joined = (
        stat_parts[:, :stat_width] + stat_parts[:, stat_width : 2 * stat_width]
    ) + stat_parts[:, 2 * stat_width : 3 * stat_width]
    returned = (
        gathered[:, :sum_width].reshape(local_rows, groups, head_width),
        joined[:, :groups],
        joined[:, groups : 2 * groups],
        gathered[:, sum_width : 2 * sum_width].reshape(local_rows, groups, head_width),
        joined[:, 2 * groups : 3 * groups],
        joined[:, 3 * groups : 4 * groups],
    )
    leaf_block = leaf_cache[:, :, 0]
    mine_queries = group_queries.reshape(local_rows, group_size, head_width)
    leaf_places = part_index * token_width + jnp.arange(token_width)
    leaf_usable = (leaf_places[None, :] < leaf_len[:, None])[:, None, :]
    leaf_scores = jnp.einsum(
        "rgd,rtd->rgt", mine_queries, leaf_block[0], preferred_element_type=jnp.float32
    ) * head_width ** (-0.5)
    leaf_partial = weigh_scores(leaf_scores, leaf_usable, leaf_block[1], "rgt,rtd->rgd")
    running = merge_partials(
        (returned[0], returned[1], returned[2]), (returned[3], returned[4], returned[5])
    )
    running = merge_partials(running, leaf_partial)
    bit_count = part_count.bit_length() - 1
    for bit_index in reversed(range(bit_count)):
        half_heads = running[1].shape[1] // 2
        upper_side = mp_index >> bit_index & 1 == 1
        kept_half = tuple(
            (
                jnp.where(upper_side, component[:, half_heads:], component[:, :half_heads])
                for component in running
            )
        )
        sent_half = tuple(
            (
                jnp.where(upper_side, component[:, :half_heads], component[:, half_heads:])
                for component in running
            )
        )
        received = partner((sent_half[0], sent_half[1], sent_half[2]), "mp", bit_index)
        running = merge_partials(kept_half, received)
    own_queries = lax.dynamic_slice_in_dim(
        queries, mp_index * own_heads * head_width, own_heads * head_width, 1
    ).reshape(local_rows, own_heads, head_width)
    fresh_kv = lax.dynamic_slice_in_dim(new_kv, kv_head * head_width, head_width, 2)
    self_score = jnp.einsum(
        "rhd,rd->rh", own_queries, fresh_kv[0], preferred_element_type=jnp.float32
    ) * head_width ** (-0.5)
    weighted, row_max, weight_total = running
    common_max = jnp.maximum(row_max, self_score)
    old_factor = jnp.exp(row_max - common_max)
    new_factor = jnp.exp(self_score - common_max)
    weighted = (
        weighted * old_factor[..., None]
        + new_factor[..., None] * fresh_kv[1].astype(jnp.float32)[:, None, :]
    )
    weight_total = weight_total * old_factor + new_factor
    attended = (
        (weighted / weight_total[..., None])
        .astype(jnp.bfloat16)
        .reshape(local_rows, own_heads * head_width)
    )
    projected = jnp.dot(attended, out_weight, preferred_element_type=jnp.float32)
    slice_width = residual.shape[1]
    mp_count = lax.axis_size("mp")
    start_col = mp_index * slice_width
    own_cols = lax.dynamic_slice_in_dim(projected, start_col, slice_width, 1) + residual.astype(
        jnp.float32
    )
    projected = lax.dynamic_update_slice_in_dim(projected, own_cols, start_col, 1)
    terms = projected.astype(jnp.bfloat16).reshape(local_rows, mp_count, slice_width)
    terms = jnp.transpose(terms, (1, 0, 2))
    received_terms = lax.all_to_all(terms, "mp", split_axis=0, concat_axis=0, tiled=True)
    kept_cols = jnp.sum(received_terms.astype(jnp.float32), axis=0)
    spread_cols = jnp.broadcast_to(
        kept_cols.astype(jnp.bfloat16)[None], (mp_count, local_rows, slice_width)
    )
    all_cols = lax.all_to_all(spread_cols, "mp", split_axis=0, concat_axis=0, tiled=True)
    hidden = jnp.transpose(all_cols, (1, 0, 2)).reshape(local_rows, -1).astype(jnp.float32)
    inv_rms = lax.rsqrt(jnp.mean(hidden * hidden, axis=1) + NORM_EPS)
    normed = (hidden * inv_rms[:, None] * norm_gain[None, :]).astype(jnp.bfloat16)
    logits = jnp.dot(normed, router, preferred_element_type=jnp.float32)
    route_hits = routes[:, :, None] == jnp.arange(EXPERTS)[None, None, :]
    chosen = jnp.sum(jnp.where(route_hits, logits[:, None, :], 0.0), axis=2)
    gate_weights = jax.nn.softmax(chosen, axis=1)
    pair_experts = routes.reshape(-1)
    pair_onehot = (pair_experts[:, None] == jnp.arange(EXPERTS)[None, :]).astype(jnp.int32)
    pair_rank = jnp.sum((jnp.cumsum(pair_onehot, axis=0) - 1) * pair_onehot, axis=1)
    pair_slot = pair_experts * E_CAP + pair_rank
    slot_source = (
        jnp.full((EXPERTS * E_CAP,), local_rows, jnp.int32)
        .at[pair_slot]
        .set(jnp.arange(pair_experts.shape[0], dtype=jnp.int32) // TOP)
    )
    padded = jnp.concatenate([normed, jnp.zeros((1, normed.shape[1]), jnp.bfloat16)], axis=0)
    local_experts = expert_in.shape[0]
    outgoing = jnp.take(padded, slot_source, axis=0).reshape(
        dp_count, local_experts, E_CAP, normed.shape[1]
    )
    returned_parts = []
    for expert_index in range(local_experts):
        incoming = lax.all_to_all(
            outgoing[:, expert_index], "dp", split_axis=0, concat_axis=0, tiled=True
        )
        gate_up = jnp.einsum(
            "scd,kfd->kscf", incoming, expert_in[expert_index], preferred_element_type=jnp.float32
        )
        expert_hidden = (jax.nn.silu(gate_up[0]) * gate_up[1]).astype(jnp.bfloat16)
        expert_partial = jnp.einsum(
            "scf,fd->scd", expert_hidden, expert_out[expert_index],
            preferred_element_type=jnp.float32,
        )
        if expert_index == local_experts - 1 and local_experts > 1:
            summed = halving_scatter(
                expert_partial.reshape(dp_count, E_CAP, mp_count, slice_width), "mp", 2
            ).astype(jnp.bfloat16)
        else:
            summed = lax.psum_scatter(
                expert_partial.astype(jnp.bfloat16), "mp", scatter_dimension=2, tiled=True
            )
        returned_parts.append(
            lax.all_to_all(summed, "dp", split_axis=0, concat_axis=0, tiled=True)
        )
    returned_rows = jnp.stack(returned_parts, axis=1)
    results = jnp.take(returned_rows.reshape(-1, slice_width), pair_slot, axis=0).reshape(
        local_rows, TOP, slice_width
    )
    layer_out = kept_cols + jnp.sum(gate_weights[:, :, None] * results.astype(jnp.float32), axis=1)
    return layer_out.astype(jnp.bfloat16)


def solution(mesh):
    placed = (
        P("dp", None),
        P(None, "dp", None),
        P("dp", "mp"),
        P("mp", None),
        P(),
        P(),
        P("dp", None, "mp", None),
        P("dp", "mp", None),
        P(None, "dp", "mp", None, None),
        P(None, "dp", "mp", None, None),
        P(),
        P(),
        P(),
        P(),
        P(),
        P(),
        P(),
        P(),
        P(),
        P("dp"),
        P("dp", None),
    )
    return jax.shard_map(
        shards, mesh=mesh, in_specs=placed, out_specs=P("dp", "mp"), check_vma=False
    )
```

```python
import jax
import jax.numpy as jnp
from jax import lax
from jax.sharding import PartitionSpec as P

HEADS = 32
KVH = 8
EXPERTS = 8
TOP = 2
PAGE = 128
ROOT_DEV = 2
BR_DEV = 8
BR_CAP = 32
E_CAP = 64


MASKED_SCORE = -1e30
NORM_EPS = 1e-05


def partner(x, axis, apart):
    return lax.ppermute(x, axis, [(i, i ^ 1 << apart) for i in range(lax.axis_size(axis))])


def merge_partials(first_part, second_part):
    first_sum, first_max, first_total = first_part
    second_sum, second_max, second_total = second_part
    common_max = jnp.maximum(first_max, second_max)
    first_factor = jnp.exp(first_max - common_max)
    second_factor = jnp.exp(second_max - common_max)
    merged_sum = first_sum * first_factor[..., None] + second_sum * second_factor[..., None]
    return (merged_sum, common_max, first_total * first_factor + second_total * second_factor)


def weigh_scores(scores, usable, values, pattern):
    masked_scores = jnp.where(usable, scores, MASKED_SCORE)
    row_max = jnp.max(masked_scores, axis=-1)
    weights = jnp.where(usable, jnp.exp(masked_scores - row_max[..., None]), 0.0)
    weight_total = jnp.sum(weights, axis=-1)
    weighted_sum = jnp.einsum(
        pattern, weights.astype(jnp.bfloat16), values, preferred_element_type=jnp.float32
    )
    return (weighted_sum, row_max, weight_total)


def shards(
    queries,
    new_kv,
    residual,
    out_weight,
    norm_gain,
    router,
    expert_in,
    expert_out,
    node_cache,
    leaf_cache,
    slot_request,
    request_branch,
    branch_parent,
    root_owner,
    branch_owner,
    root_pages,
    branch_pages,
    root_len,
    branch_len,
    leaf_len,
    routes,
):
    head_width = node_cache.shape[-1]
    token_width = node_cache.shape[-2]
    part_count = lax.axis_size("mp") // KVH
    group_size = HEADS // KVH
    own_heads = HEADS // lax.axis_size("mp")
    local_rows = queries.shape[0]
    requests = slot_request.shape[0]
    branches = branch_parent.shape[0]
    root_count = root_owner.shape[0]
    mp_index = lax.axis_index("mp")
    dp_index = lax.axis_index("dp")
    kv_head = mp_index // part_count
    part_index = mp_index % part_count
    group_queries = lax.dynamic_slice_in_dim(
        queries, kv_head * group_size * head_width, group_size * head_width, 1
    )
    dp_count = lax.axis_size("dp")
    all_queries = lax.all_to_all(
        jnp.broadcast_to(group_queries[None], (dp_count,) + group_queries.shape),
        "dp",
        split_axis=0,
        concat_axis=0,
        tiled=True,
    ).reshape(requests, group_size, head_width)
    slot_branch = jnp.sum(
        jnp.where(
            slot_request[:, None] == jnp.arange(requests)[None, :], request_branch[None, :], 0
        ),
        axis=1,
    )
    slot_root = jnp.sum(
        jnp.where(
            slot_branch[:, None] == jnp.arange(branches)[None, :], branch_parent[None, :], 0
        ),
        axis=1,
    )
    local_roots = jnp.nonzero(root_owner == dp_index, size=ROOT_DEV)[0]
    local_branches = jnp.nonzero(branch_owner == dp_index, size=BR_DEV)[0]
    page_pool = node_cache[:, :, 0]
    flat_queries = all_queries.reshape(requests, group_size * head_width)

    def selection(node_of_slot, nodes, cap):
        hit = node_of_slot[None, :] == nodes[:, None]
        rank = jnp.cumsum(hit.astype(jnp.int32), axis=1) - 1
        return hit[:, None, :] & (rank[:, None, :] == jnp.arange(cap)[None, :, None])

    def level_rows(nodes, node_pages, node_len, cap):
        pick = selection(node_of_slot_for[cap], nodes, cap)
        member_queries = jnp.einsum(
            "nks,sx->nkx", pick.astype(jnp.bfloat16), flat_queries,
            preferred_element_type=jnp.float32,
        ).astype(jnp.bfloat16).reshape(nodes.shape[0], cap, group_size, head_width)
        page_list = jnp.take(node_pages, nodes, axis=0)
        blocks = jnp.take(page_pool, page_list.reshape(-1), axis=1).reshape(
            (2,) + page_list.shape + page_pool.shape[2:]
        )
        lengths = jnp.take(node_len, nodes)

        def one_node(queries_of, keys_of, values_of, length):
            page_count = keys_of.shape[0]
            positions = (
                jnp.arange(page_count)[:, None] * PAGE
                + part_index * token_width
                + jnp.arange(token_width)[None, :]
            ).reshape(-1)
            usable = (positions < length)[None, None, :]
            scores = jnp.einsum(
                "sgd,ld->sgl", queries_of, keys_of.reshape(-1, head_width),
                preferred_element_type=jnp.float32,
            ) * head_width ** (-0.5)
            return weigh_scores(scores, usable, values_of.reshape(-1, head_width), "sgl,ld->sgd")

        weighted_sum, row_max, weight_total = jax.vmap(one_node)(
            member_queries, blocks[0], blocks[1], lengths
        )
        stats = jnp.concatenate([row_max, weight_total], axis=2)
        stats = jnp.pad(stats, ((0, 0), (0, 0), (0, head_width - 2 * group_size)))
        rows = jnp.concatenate(
            [weighted_sum.reshape(nodes.shape[0], cap, group_size * head_width), stats], axis=2
        )
        return jnp.einsum(
            "nks,nkc->sc", pick.astype(jnp.float32), rows,
            precision=lax.Precision.HIGHEST, preferred_element_type=jnp.float32,
        )

    root_cap = (branches // root_count) * BR_CAP
    node_of_slot_for = {root_cap: slot_root, BR_CAP: slot_branch}
    root_rows = level_rows(local_roots, root_pages, root_len, root_cap)
    branch_rows = level_rows(local_branches, branch_pages, branch_len, BR_CAP)
    groups = group_size
    dp_count = lax.axis_size("dp")
    stats = jnp.concatenate(
        [root_rows[:, groups * head_width : (groups * head_width + 2 * groups)],
         branch_rows[:, groups * head_width : (groups * head_width + 2 * groups)]],
        axis=1,
    )
    stats_high = lax.reduce_precision(stats, exponent_bits=8, mantissa_bits=7)
    stats_rest = stats - stats_high
    stats_mid = lax.reduce_precision(stats_rest, exponent_bits=8, mantissa_bits=7)
    stats_low = stats_rest - stats_mid
    stat_block = jnp.concatenate([stats_high, stats_mid, stats_low], axis=1).astype(jnp.bfloat16)
    stat_block = jnp.pad(stat_block, ((0, 0), (0, head_width - stat_block.shape[1])))
    packed = jnp.concatenate(
        [root_rows[:, : groups * head_width].astype(jnp.bfloat16),
         branch_rows[:, : groups * head_width].astype(jnp.bfloat16),
         stat_block],
        axis=1,
    )
    exchanged = lax.all_to_all(
        packed.reshape(dp_count, local_rows, packed.shape[1]),
        "dp",
        split_axis=0,
        concat_axis=0,
        tiled=True,
    )
    gathered = jnp.sum(exchanged.astype(jnp.float32), axis=0)
    sum_width = groups * head_width
    stat_width = 4 * groups
    stat_parts = gathered[:, 2 * sum_width :]
    joined = (
        stat_parts[:, :stat_width] + stat_parts[:, stat_width : 2 * stat_width]
    ) + stat_parts[:, 2 * stat_width : 3 * stat_width]
    returned = (
        gathered[:, :sum_width].reshape(local_rows, groups, head_width),
        joined[:, :groups],
        joined[:, groups : 2 * groups],
        gathered[:, sum_width : 2 * sum_width].reshape(local_rows, groups, head_width),
        joined[:, 2 * groups : 3 * groups],
        joined[:, 3 * groups : 4 * groups],
    )
    leaf_block = leaf_cache[:, :, 0]
    mine_queries = group_queries.reshape(local_rows, group_size, head_width)
    leaf_places = part_index * token_width + jnp.arange(token_width)
    leaf_usable = (leaf_places[None, :] < leaf_len[:, None])[:, None, :]
    leaf_scores = jnp.einsum(
        "rgd,rtd->rgt", mine_queries, leaf_block[0], preferred_element_type=jnp.float32
    ) * head_width ** (-0.5)
    leaf_partial = weigh_scores(leaf_scores, leaf_usable, leaf_block[1], "rgt,rtd->rgd")
    running = merge_partials(
        (returned[0], returned[1], returned[2]), (returned[3], returned[4], returned[5])
    )
    running = merge_partials(running, leaf_partial)
    bit_count = part_count.bit_length() - 1
    for bit_index in reversed(range(bit_count)):
        half_heads = running[1].shape[1] // 2
        upper_side = mp_index >> bit_index & 1 == 1
        kept_half = tuple(
            (
                jnp.where(upper_side, component[:, half_heads:], component[:, :half_heads])
                for component in running
            )
        )
        sent_half = tuple(
            (
                jnp.where(upper_side, component[:, :half_heads], component[:, half_heads:])
                for component in running
            )
        )
        received = partner((sent_half[0], sent_half[1], sent_half[2]), "mp", bit_index)
        running = merge_partials(kept_half, received)
    own_queries = lax.dynamic_slice_in_dim(
        queries, mp_index * own_heads * head_width, own_heads * head_width, 1
    ).reshape(local_rows, own_heads, head_width)
    fresh_kv = lax.dynamic_slice_in_dim(new_kv, kv_head * head_width, head_width, 2)
    self_score = jnp.einsum(
        "rhd,rd->rh", own_queries, fresh_kv[0], preferred_element_type=jnp.float32
    ) * head_width ** (-0.5)
    weighted, row_max, weight_total = running
    common_max = jnp.maximum(row_max, self_score)
    old_factor = jnp.exp(row_max - common_max)
    new_factor = jnp.exp(self_score - common_max)
    weighted = (
        weighted * old_factor[..., None]
        + new_factor[..., None] * fresh_kv[1].astype(jnp.float32)[:, None, :]
    )
    weight_total = weight_total * old_factor + new_factor
    attended = (
        (weighted / weight_total[..., None])
        .astype(jnp.bfloat16)
        .reshape(local_rows, own_heads * head_width)
    )
    projected = jnp.dot(attended, out_weight, preferred_element_type=jnp.float32)
    slice_width = residual.shape[1]
    mp_count = lax.axis_size("mp")
    start_col = mp_index * slice_width
    own_cols = lax.dynamic_slice_in_dim(projected, start_col, slice_width, 1) + residual.astype(
        jnp.float32
    )
    projected = lax.dynamic_update_slice_in_dim(projected, own_cols, start_col, 1)
    terms = projected.astype(jnp.bfloat16).reshape(local_rows, mp_count, slice_width)
    terms = jnp.transpose(terms, (1, 0, 2))
    received_terms = lax.all_to_all(terms, "mp", split_axis=0, concat_axis=0, tiled=True)
    kept_cols = jnp.sum(received_terms.astype(jnp.float32), axis=0)
    spread_cols = jnp.broadcast_to(
        kept_cols.astype(jnp.bfloat16)[None], (mp_count, local_rows, slice_width)
    )
    all_cols = lax.all_to_all(spread_cols, "mp", split_axis=0, concat_axis=0, tiled=True)
    hidden = jnp.transpose(all_cols, (1, 0, 2)).reshape(local_rows, -1).astype(jnp.float32)
    inv_rms = lax.rsqrt(jnp.mean(hidden * hidden, axis=1) + NORM_EPS)
    normed = (hidden * inv_rms[:, None] * norm_gain[None, :]).astype(jnp.bfloat16)
    logits = jnp.dot(normed, router, preferred_element_type=jnp.float32)
    route_hits = routes[:, :, None] == jnp.arange(EXPERTS)[None, None, :]
    chosen = jnp.sum(jnp.where(route_hits, logits[:, None, :], 0.0), axis=2)
    gate_weights = jax.nn.softmax(chosen, axis=1)
    pair_experts = routes.reshape(-1)
    pair_onehot = (pair_experts[:, None] == jnp.arange(EXPERTS)[None, :]).astype(jnp.int32)
    pair_rank = jnp.sum((jnp.cumsum(pair_onehot, axis=0) - 1) * pair_onehot, axis=1)
    pair_slot = pair_experts * E_CAP + pair_rank
    slot_source = (
        jnp.full((EXPERTS * E_CAP,), local_rows, jnp.int32)
        .at[pair_slot]
        .set(jnp.arange(pair_experts.shape[0], dtype=jnp.int32) // TOP)
    )
    padded = jnp.concatenate([normed, jnp.zeros((1, normed.shape[1]), jnp.bfloat16)], axis=0)
    local_experts = expert_in.shape[0]
    outgoing = jnp.take(padded, slot_source, axis=0).reshape(
        dp_count, local_experts, E_CAP, normed.shape[1]
    )
    returned_parts = []
    for expert_index in range(local_experts):
        incoming = lax.all_to_all(
            outgoing[:, expert_index], "dp", split_axis=0, concat_axis=0, tiled=True
        )
        gate_up = jnp.einsum(
            "scd,kfd->kscf", incoming, expert_in[expert_index], preferred_element_type=jnp.float32
        )
        expert_hidden = (jax.nn.silu(gate_up[0]) * gate_up[1]).astype(jnp.bfloat16)
        if expert_index == local_experts - 1 and local_experts > 1:
            pieces = jnp.einsum(
                "scf,fmd->mscd", expert_hidden,
                expert_out[expert_index].reshape(-1, mp_count, slice_width),
                preferred_element_type=jnp.float32,
            ).astype(jnp.bfloat16)
            gathered_pieces = lax.all_to_all(pieces, "mp", split_axis=0, concat_axis=0, tiled=True)
            summed = jnp.sum(gathered_pieces.astype(jnp.float32), axis=0).astype(jnp.bfloat16)
        else:
            expert_partial = jnp.einsum(
                "scf,fd->scd", expert_hidden, expert_out[expert_index],
                preferred_element_type=jnp.float32,
            )
            summed = lax.psum_scatter(
                expert_partial.astype(jnp.bfloat16), "mp", scatter_dimension=2, tiled=True
            )
        returned_parts.append(summed)
    returned_rows = lax.all_to_all(
        jnp.stack(returned_parts, axis=1), "dp", split_axis=0, concat_axis=0, tiled=True
    )
    results = jnp.take(returned_rows.reshape(-1, slice_width), pair_slot, axis=0).reshape(
        local_rows, TOP, slice_width
    )
    layer_out = kept_cols + jnp.sum(gate_weights[:, :, None] * results.astype(jnp.float32), axis=1)
    return layer_out.astype(jnp.bfloat16)


def solution(mesh):
    placed = (
        P("dp", None),
        P(None, "dp", None),
        P("dp", "mp"),
        P("mp", None),
        P(),
        P(),
        P("dp", None, "mp", None),
        P("dp", "mp", None),
        P(None, "dp", "mp", None, None),
        P(None, "dp", "mp", None, None),
        P(),
        P(),
        P(),
        P(),
        P(),
        P(),
        P(),
        P(),
        P(),
        P("dp"),
        P("dp", None),
    )
    return jax.shard_map(
        shards, mesh=mesh, in_specs=placed, out_specs=P("dp", "mp"), check_vma=False
    )
```

```python
import jax
import jax.numpy as jnp
from jax import lax
from jax.sharding import PartitionSpec as P

HEADS = 32
KVH = 8
EXPERTS = 8
TOP = 2
PAGE = 128
ROOT_DEV = 2
BR_DEV = 8
BR_CAP = 32
E_CAP = 64


MASKED_SCORE = -1e30
NORM_EPS = 1e-05


def partner(x, axis, apart):
    return lax.ppermute(x, axis, [(i, i ^ 1 << apart) for i in range(lax.axis_size(axis))])


def merge_partials(first_part, second_part):
    first_sum, first_max, first_total = first_part
    second_sum, second_max, second_total = second_part
    common_max = jnp.maximum(first_max, second_max)
    first_factor = jnp.exp(first_max - common_max)
    second_factor = jnp.exp(second_max - common_max)
    merged_sum = first_sum * first_factor[..., None] + second_sum * second_factor[..., None]
    return (merged_sum, common_max, first_total * first_factor + second_total * second_factor)


def weigh_scores(scores, usable, values, pattern):
    masked_scores = jnp.where(usable, scores, MASKED_SCORE)
    row_max = jnp.max(masked_scores, axis=-1)
    weights = jnp.where(usable, jnp.exp(masked_scores - row_max[..., None]), 0.0)
    weight_total = jnp.sum(weights, axis=-1)
    weighted_sum = jnp.einsum(
        pattern, weights.astype(jnp.bfloat16), values, preferred_element_type=jnp.float32
    )
    return (weighted_sum, row_max, weight_total)


def shards(
    queries,
    new_kv,
    residual,
    out_weight,
    norm_gain,
    router,
    expert_in,
    expert_out,
    node_cache,
    leaf_cache,
    slot_request,
    request_branch,
    branch_parent,
    root_owner,
    branch_owner,
    root_pages,
    branch_pages,
    root_len,
    branch_len,
    leaf_len,
    routes,
):
    head_width = node_cache.shape[-1]
    token_width = node_cache.shape[-2]
    part_count = lax.axis_size("mp") // KVH
    group_size = HEADS // KVH
    own_heads = HEADS // lax.axis_size("mp")
    local_rows = queries.shape[0]
    requests = slot_request.shape[0]
    branches = branch_parent.shape[0]
    root_count = root_owner.shape[0]
    mp_index = lax.axis_index("mp")
    dp_index = lax.axis_index("dp")
    kv_head = mp_index // part_count
    part_index = mp_index % part_count
    group_queries = lax.dynamic_slice_in_dim(
        queries, kv_head * group_size * head_width, group_size * head_width, 1
    )
    dp_count = lax.axis_size("dp")
    all_queries = lax.all_to_all(
        jnp.broadcast_to(group_queries[None], (dp_count,) + group_queries.shape),
        "dp",
        split_axis=0,
        concat_axis=0,
        tiled=True,
    ).reshape(requests, group_size, head_width)
    slot_branch = jnp.sum(
        jnp.where(
            slot_request[:, None] == jnp.arange(requests)[None, :], request_branch[None, :], 0
        ),
        axis=1,
    )
    slot_root = jnp.sum(
        jnp.where(
            slot_branch[:, None] == jnp.arange(branches)[None, :], branch_parent[None, :], 0
        ),
        axis=1,
    )
    local_roots = jnp.nonzero(root_owner == dp_index, size=ROOT_DEV)[0]
    local_branches = jnp.nonzero(branch_owner == dp_index, size=BR_DEV)[0]
    page_pool = node_cache[:, :, 0]
    flat_queries = all_queries.reshape(requests, group_size * head_width)

    def selection(node_of_slot, nodes, cap):
        hit = node_of_slot[None, :] == nodes[:, None]
        rank = jnp.cumsum(hit.astype(jnp.int32), axis=1) - 1
        return hit[:, None, :] & (rank[:, None, :] == jnp.arange(cap)[None, :, None])

    def level_rows(nodes, node_pages, node_len, cap):
        pick = selection(node_of_slot_for[cap], nodes, cap)
        member_queries = jnp.einsum(
            "nks,sx->nkx", pick.astype(jnp.bfloat16), flat_queries,
            preferred_element_type=jnp.float32,
        ).astype(jnp.bfloat16).reshape(nodes.shape[0], cap, group_size, head_width)
        page_list = jnp.take(node_pages, nodes, axis=0)
        blocks = jnp.take(page_pool, page_list.reshape(-1), axis=1).reshape(
            (2,) + page_list.shape + page_pool.shape[2:]
        )
        lengths = jnp.take(node_len, nodes)

        def one_node(queries_of, keys_of, values_of, length):
            page_count = keys_of.shape[0]
            positions = (
                jnp.arange(page_count)[:, None] * PAGE
                + part_index * token_width
                + jnp.arange(token_width)[None, :]
            ).reshape(-1)
            usable = (positions < length)[None, None, :]
            scores = jnp.einsum(
                "sgd,ld->sgl", queries_of, keys_of.reshape(-1, head_width),
                preferred_element_type=jnp.float32,
            ) * head_width ** (-0.5)
            return weigh_scores(scores, usable, values_of.reshape(-1, head_width), "sgl,ld->sgd")

        weighted_sum, row_max, weight_total = jax.vmap(one_node)(
            member_queries, blocks[0], blocks[1], lengths
        )
        stats = jnp.concatenate([row_max, weight_total], axis=2)
        stats = jnp.pad(stats, ((0, 0), (0, 0), (0, head_width - 2 * group_size)))
        rows = jnp.concatenate(
            [weighted_sum.reshape(nodes.shape[0], cap, group_size * head_width), stats], axis=2
        )
        return jnp.einsum(
            "nks,nkc->sc", pick.astype(jnp.float32), rows,
            precision=lax.Precision.HIGHEST, preferred_element_type=jnp.float32,
        )

    root_cap = (branches // root_count) * BR_CAP
    node_of_slot_for = {root_cap: slot_root, BR_CAP: slot_branch}
    root_rows = level_rows(local_roots, root_pages, root_len, root_cap)
    branch_rows = level_rows(local_branches, branch_pages, branch_len, BR_CAP)
    groups = group_size
    dp_count = lax.axis_size("dp")
    stats = jnp.concatenate(
        [root_rows[:, groups * head_width : (groups * head_width + 2 * groups)],
         branch_rows[:, groups * head_width : (groups * head_width + 2 * groups)]],
        axis=1,
    )
    stats_high = lax.reduce_precision(stats, exponent_bits=8, mantissa_bits=7)
    stats_rest = stats - stats_high
    stats_mid = lax.reduce_precision(stats_rest, exponent_bits=8, mantissa_bits=7)
    stats_low = stats_rest - stats_mid
    stat_block = jnp.concatenate([stats_high, stats_mid, stats_low], axis=1).astype(jnp.bfloat16)
    stat_block = jnp.pad(stat_block, ((0, 0), (0, head_width - stat_block.shape[1])))
    packed = jnp.concatenate(
        [root_rows[:, : groups * head_width].astype(jnp.bfloat16),
         branch_rows[:, : groups * head_width].astype(jnp.bfloat16),
         stat_block],
        axis=1,
    )
    exchanged = lax.all_to_all(
        packed.reshape(dp_count, local_rows, packed.shape[1]),
        "dp",
        split_axis=0,
        concat_axis=0,
        tiled=True,
    )
    gathered = jnp.sum(exchanged.astype(jnp.float32), axis=0)
    sum_width = groups * head_width
    stat_width = 4 * groups
    stat_parts = gathered[:, 2 * sum_width :]
    joined = (
        stat_parts[:, :stat_width] + stat_parts[:, stat_width : 2 * stat_width]
    ) + stat_parts[:, 2 * stat_width : 3 * stat_width]
    returned = (
        gathered[:, :sum_width].reshape(local_rows, groups, head_width),
        joined[:, :groups],
        joined[:, groups : 2 * groups],
        gathered[:, sum_width : 2 * sum_width].reshape(local_rows, groups, head_width),
        joined[:, 2 * groups : 3 * groups],
        joined[:, 3 * groups : 4 * groups],
    )
    leaf_block = leaf_cache[:, :, 0]
    mine_queries = group_queries.reshape(local_rows, group_size, head_width)
    leaf_places = part_index * token_width + jnp.arange(token_width)
    leaf_usable = (leaf_places[None, :] < leaf_len[:, None])[:, None, :]
    leaf_scores = jnp.einsum(
        "rgd,rtd->rgt", mine_queries, leaf_block[0], preferred_element_type=jnp.float32
    ) * head_width ** (-0.5)
    leaf_partial = weigh_scores(leaf_scores, leaf_usable, leaf_block[1], "rgt,rtd->rgd")
    running = merge_partials(
        (returned[0], returned[1], returned[2]), (returned[3], returned[4], returned[5])
    )
    running = merge_partials(running, leaf_partial)
    bit_count = part_count.bit_length() - 1
    for bit_index in reversed(range(bit_count)):
        half_heads = running[1].shape[1] // 2
        upper_side = mp_index >> bit_index & 1 == 1
        kept_half = tuple(
            (
                jnp.where(upper_side, component[:, half_heads:], component[:, :half_heads])
                for component in running
            )
        )
        sent_half = tuple(
            (
                jnp.where(upper_side, component[:, :half_heads], component[:, half_heads:])
                for component in running
            )
        )
        received = partner((sent_half[0], sent_half[1], sent_half[2]), "mp", bit_index)
        running = merge_partials(kept_half, received)
    own_queries = lax.dynamic_slice_in_dim(
        queries, mp_index * own_heads * head_width, own_heads * head_width, 1
    ).reshape(local_rows, own_heads, head_width)
    fresh_kv = lax.dynamic_slice_in_dim(new_kv, kv_head * head_width, head_width, 2)
    self_score = jnp.einsum(
        "rhd,rd->rh", own_queries, fresh_kv[0], preferred_element_type=jnp.float32
    ) * head_width ** (-0.5)
    weighted, row_max, weight_total = running
    common_max = jnp.maximum(row_max, self_score)
    old_factor = jnp.exp(row_max - common_max)
    new_factor = jnp.exp(self_score - common_max)
    weighted = (
        weighted * old_factor[..., None]
        + new_factor[..., None] * fresh_kv[1].astype(jnp.float32)[:, None, :]
    )
    weight_total = weight_total * old_factor + new_factor
    attended = (
        (weighted / weight_total[..., None])
        .astype(jnp.bfloat16)
        .reshape(local_rows, own_heads * head_width)
    )
    projected = jnp.dot(attended, out_weight, preferred_element_type=jnp.float32)
    slice_width = residual.shape[1]
    mp_count = lax.axis_size("mp")
    start_col = mp_index * slice_width
    own_cols = lax.dynamic_slice_in_dim(projected, start_col, slice_width, 1) + residual.astype(
        jnp.float32
    )
    projected = lax.dynamic_update_slice_in_dim(projected, own_cols, start_col, 1)
    terms = projected.astype(jnp.bfloat16).reshape(local_rows, mp_count, slice_width)
    terms = jnp.transpose(terms, (1, 0, 2))
    received_terms = lax.all_to_all(terms, "mp", split_axis=0, concat_axis=0, tiled=True)
    kept_cols = jnp.sum(received_terms.astype(jnp.float32), axis=0)
    spread_cols = jnp.broadcast_to(
        kept_cols.astype(jnp.bfloat16)[None], (mp_count, local_rows, slice_width)
    )
    all_cols = lax.all_to_all(spread_cols, "mp", split_axis=0, concat_axis=0, tiled=True)
    hidden = jnp.transpose(all_cols, (1, 0, 2)).reshape(local_rows, -1).astype(jnp.float32)
    inv_rms = lax.rsqrt(jnp.mean(hidden * hidden, axis=1) + NORM_EPS)
    normed = (hidden * inv_rms[:, None] * norm_gain[None, :]).astype(jnp.bfloat16)
    logits = jnp.dot(normed, router, preferred_element_type=jnp.float32)
    route_hits = routes[:, :, None] == jnp.arange(EXPERTS)[None, None, :]
    chosen = jnp.sum(jnp.where(route_hits, logits[:, None, :], 0.0), axis=2)
    gate_weights = jax.nn.softmax(chosen, axis=1)
    pair_experts = routes.reshape(-1)
    pair_onehot = (pair_experts[:, None] == jnp.arange(EXPERTS)[None, :]).astype(jnp.int32)
    pair_rank = jnp.sum((jnp.cumsum(pair_onehot, axis=0) - 1) * pair_onehot, axis=1)
    pair_slot = pair_experts * E_CAP + pair_rank
    slot_source = (
        jnp.full((EXPERTS * E_CAP,), local_rows, jnp.int32)
        .at[pair_slot]
        .set(jnp.arange(pair_experts.shape[0], dtype=jnp.int32) // TOP)
    )
    padded = jnp.concatenate([normed, jnp.zeros((1, normed.shape[1]), jnp.bfloat16)], axis=0)
    local_experts = expert_in.shape[0]
    outgoing = jnp.take(padded, slot_source, axis=0).reshape(
        dp_count, local_experts, E_CAP, normed.shape[1]
    )
    returned_parts = []
    for expert_index in range(local_experts):
        incoming = lax.all_to_all(
            outgoing[:, expert_index], "dp", split_axis=0, concat_axis=0, tiled=True
        )
        gate_up = jnp.einsum(
            "scd,kfd->kscf", incoming, expert_in[expert_index], preferred_element_type=jnp.float32
        )
        expert_hidden = (jax.nn.silu(gate_up[0]) * gate_up[1]).astype(jnp.bfloat16)
        if expert_index == local_experts - 1 and local_experts > 1:
            pieces = jnp.einsum(
                "scf,fmd->mscd", expert_hidden,
                expert_out[expert_index].reshape(-1, mp_count, slice_width),
                preferred_element_type=jnp.float32,
            ).astype(jnp.bfloat16)
            gathered_pieces = lax.all_to_all(pieces, "mp", split_axis=0, concat_axis=0, tiled=True)
            summed = jnp.sum(gathered_pieces.astype(jnp.float32), axis=0).astype(jnp.bfloat16)
        else:
            expert_partial = jnp.einsum(
                "scf,fd->scd", expert_hidden, expert_out[expert_index],
                preferred_element_type=jnp.float32,
            )
            summed = lax.psum_scatter(
                expert_partial.astype(jnp.bfloat16), "mp", scatter_dimension=2, tiled=True
            )
        returned_parts.append(
            lax.all_to_all(summed, "dp", split_axis=0, concat_axis=0, tiled=True)
        )
    returned_rows = jnp.stack(returned_parts, axis=1)
    results = jnp.take(returned_rows.reshape(-1, slice_width), pair_slot, axis=0).reshape(
        local_rows, TOP, slice_width
    )
    layer_out = kept_cols + jnp.sum(gate_weights[:, :, None] * results.astype(jnp.float32), axis=1)
    return layer_out.astype(jnp.bfloat16)


def solution(mesh):
    placed = (
        P("dp", None),
        P(None, "dp", None),
        P("dp", "mp"),
        P("mp", None),
        P(),
        P(),
        P("dp", None, "mp", None),
        P("dp", "mp", None),
        P(None, "dp", "mp", None, None),
        P(None, "dp", "mp", None, None),
        P(),
        P(),
        P(),
        P(),
        P(),
        P(),
        P(),
        P(),
        P(),
        P("dp"),
        P("dp", None),
    )
    return jax.shard_map(
        shards, mesh=mesh, in_specs=placed, out_specs=P("dp", "mp"), check_vma=False
    )
```

```python
import jax
import jax.numpy as jnp
from jax import lax
from jax.sharding import PartitionSpec as P

HEADS = 32
KVH = 8
EXPERTS = 8
TOP = 2
PAGE = 128
ROOT_DEV = 2
BR_DEV = 8
BR_CAP = 32
E_CAP = 64


MASKED_SCORE = -1e30
NORM_EPS = 1e-05


def partner(x, axis, apart):
    return lax.ppermute(x, axis, [(i, i ^ 1 << apart) for i in range(lax.axis_size(axis))])


def merge_partials(first_part, second_part):
    first_sum, first_max, first_total = first_part
    second_sum, second_max, second_total = second_part
    common_max = jnp.maximum(first_max, second_max)
    first_factor = jnp.exp(first_max - common_max)
    second_factor = jnp.exp(second_max - common_max)
    merged_sum = first_sum * first_factor[..., None] + second_sum * second_factor[..., None]
    return (merged_sum, common_max, first_total * first_factor + second_total * second_factor)


def weigh_scores(scores, usable, values, pattern):
    masked_scores = jnp.where(usable, scores, MASKED_SCORE)
    row_max = jnp.max(masked_scores, axis=-1)
    weights = jnp.where(usable, jnp.exp(masked_scores - row_max[..., None]), 0.0)
    weight_total = jnp.sum(weights, axis=-1)
    weighted_sum = jnp.einsum(
        pattern, weights.astype(jnp.bfloat16), values, preferred_element_type=jnp.float32
    )
    return (weighted_sum, row_max, weight_total)


def shards(
    queries,
    new_kv,
    residual,
    out_weight,
    norm_gain,
    router,
    expert_in,
    expert_out,
    node_cache,
    leaf_cache,
    slot_request,
    request_branch,
    branch_parent,
    root_owner,
    branch_owner,
    root_pages,
    branch_pages,
    root_len,
    branch_len,
    leaf_len,
    routes,
):
    head_width = node_cache.shape[-1]
    token_width = node_cache.shape[-2]
    part_count = lax.axis_size("mp") // KVH
    group_size = HEADS // KVH
    own_heads = HEADS // lax.axis_size("mp")
    local_rows = queries.shape[0]
    requests = slot_request.shape[0]
    branches = branch_parent.shape[0]
    root_count = root_owner.shape[0]
    mp_index = lax.axis_index("mp")
    dp_index = lax.axis_index("dp")
    kv_head = mp_index // part_count
    part_index = mp_index % part_count
    group_queries = lax.dynamic_slice_in_dim(
        queries, kv_head * group_size * head_width, group_size * head_width, 1
    )
    all_queries = lax.all_gather(group_queries, "dp", axis=0, tiled=True).reshape(
        requests, group_size, head_width
    )
    slot_branch = jnp.sum(
        jnp.where(
            slot_request[:, None] == jnp.arange(requests)[None, :], request_branch[None, :], 0
        ),
        axis=1,
    )
    slot_root = jnp.sum(
        jnp.where(
            slot_branch[:, None] == jnp.arange(branches)[None, :], branch_parent[None, :], 0
        ),
        axis=1,
    )
    local_roots = jnp.nonzero(root_owner == dp_index, size=ROOT_DEV)[0]
    local_branches = jnp.nonzero(branch_owner == dp_index, size=BR_DEV)[0]
    page_pool = node_cache[:, :, 0]
    flat_queries = all_queries.reshape(requests, group_size * head_width)

    def selection(node_of_slot, nodes, cap):
        hit = node_of_slot[None, :] == nodes[:, None]
        rank = jnp.cumsum(hit.astype(jnp.int32), axis=1) - 1
        return hit[:, None, :] & (rank[:, None, :] == jnp.arange(cap)[None, :, None])

    def level_rows(nodes, node_pages, node_len, cap):
        pick = selection(node_of_slot_for[cap], nodes, cap)
        member_queries = jnp.einsum(
            "nks,sx->nkx", pick.astype(jnp.bfloat16), flat_queries,
            preferred_element_type=jnp.float32,
        ).astype(jnp.bfloat16).reshape(nodes.shape[0], cap, group_size, head_width)
        page_list = jnp.take(node_pages, nodes, axis=0)
        blocks = jnp.take(page_pool, page_list.reshape(-1), axis=1).reshape(
            (2,) + page_list.shape + page_pool.shape[2:]
        )
        lengths = jnp.take(node_len, nodes)

        def one_node(queries_of, keys_of, values_of, length):
            page_count = keys_of.shape[0]
            positions = (
                jnp.arange(page_count)[:, None] * PAGE
                + part_index * token_width
                + jnp.arange(token_width)[None, :]
            ).reshape(-1)
            usable = (positions < length)[None, None, :]
            scores = jnp.einsum(
                "sgd,ld->sgl", queries_of, keys_of.reshape(-1, head_width),
                preferred_element_type=jnp.float32,
            ) * head_width ** (-0.5)
            return weigh_scores(scores, usable, values_of.reshape(-1, head_width), "sgl,ld->sgd")

        weighted_sum, row_max, weight_total = jax.vmap(one_node)(
            member_queries, blocks[0], blocks[1], lengths
        )
        stats = jnp.concatenate([row_max, weight_total], axis=2)
        stats = jnp.pad(stats, ((0, 0), (0, 0), (0, head_width - 2 * group_size)))
        rows = jnp.concatenate(
            [weighted_sum.reshape(nodes.shape[0], cap, group_size * head_width), stats], axis=2
        )
        return jnp.einsum(
            "nks,nkc->sc", pick.astype(jnp.float32), rows,
            precision=lax.Precision.HIGHEST, preferred_element_type=jnp.float32,
        )

    root_cap = (branches // root_count) * BR_CAP
    node_of_slot_for = {root_cap: slot_root, BR_CAP: slot_branch}
    root_rows = level_rows(local_roots, root_pages, root_len, root_cap)
    branch_rows = level_rows(local_branches, branch_pages, branch_len, BR_CAP)
    groups = group_size
    dp_count = lax.axis_size("dp")
    stats = jnp.concatenate(
        [root_rows[:, groups * head_width : (groups * head_width + 2 * groups)],
         branch_rows[:, groups * head_width : (groups * head_width + 2 * groups)]],
        axis=1,
    )
    stats_high = lax.reduce_precision(stats, exponent_bits=8, mantissa_bits=7)
    stats_rest = stats - stats_high
    stats_mid = lax.reduce_precision(stats_rest, exponent_bits=8, mantissa_bits=7)
    stats_low = stats_rest - stats_mid
    stat_block = jnp.concatenate([stats_high, stats_mid, stats_low], axis=1).astype(jnp.bfloat16)
    stat_block = jnp.pad(stat_block, ((0, 0), (0, head_width - stat_block.shape[1])))
    packed = jnp.concatenate(
        [root_rows[:, : groups * head_width].astype(jnp.bfloat16),
         branch_rows[:, : groups * head_width].astype(jnp.bfloat16),
         stat_block],
        axis=1,
    )
    exchanged = lax.all_to_all(
        packed.reshape(dp_count, local_rows, packed.shape[1]),
        "dp",
        split_axis=0,
        concat_axis=0,
        tiled=True,
    )
    gathered = jnp.sum(exchanged.astype(jnp.float32), axis=0)
    sum_width = groups * head_width
    stat_width = 4 * groups
    stat_parts = gathered[:, 2 * sum_width :]
    joined = (
        stat_parts[:, :stat_width] + stat_parts[:, stat_width : 2 * stat_width]
    ) + stat_parts[:, 2 * stat_width : 3 * stat_width]
    returned = (
        gathered[:, :sum_width].reshape(local_rows, groups, head_width),
        joined[:, :groups],
        joined[:, groups : 2 * groups],
        gathered[:, sum_width : 2 * sum_width].reshape(local_rows, groups, head_width),
        joined[:, 2 * groups : 3 * groups],
        joined[:, 3 * groups : 4 * groups],
    )
    leaf_block = leaf_cache[:, :, 0]
    mine_queries = group_queries.reshape(local_rows, group_size, head_width)
    leaf_places = part_index * token_width + jnp.arange(token_width)
    leaf_usable = (leaf_places[None, :] < leaf_len[:, None])[:, None, :]
    leaf_scores = jnp.einsum(
        "rgd,rtd->rgt", mine_queries, leaf_block[0], preferred_element_type=jnp.float32
    ) * head_width ** (-0.5)
    leaf_partial = weigh_scores(leaf_scores, leaf_usable, leaf_block[1], "rgt,rtd->rgd")
    running = merge_partials(
        (returned[0], returned[1], returned[2]), (returned[3], returned[4], returned[5])
    )
    running = merge_partials(running, leaf_partial)
    bit_count = part_count.bit_length() - 1
    for bit_index in reversed(range(bit_count)):
        half_heads = running[1].shape[1] // 2
        upper_side = mp_index >> bit_index & 1 == 1
        kept_half = tuple(
            (
                jnp.where(upper_side, component[:, half_heads:], component[:, :half_heads])
                for component in running
            )
        )
        sent_half = tuple(
            (
                jnp.where(upper_side, component[:, :half_heads], component[:, half_heads:])
                for component in running
            )
        )
        received = partner((sent_half[0], sent_half[1], sent_half[2]), "mp", bit_index)
        running = merge_partials(kept_half, received)
    own_queries = lax.dynamic_slice_in_dim(
        queries, mp_index * own_heads * head_width, own_heads * head_width, 1
    ).reshape(local_rows, own_heads, head_width)
    fresh_kv = lax.dynamic_slice_in_dim(new_kv, kv_head * head_width, head_width, 2)
    self_score = jnp.einsum(
        "rhd,rd->rh", own_queries, fresh_kv[0], preferred_element_type=jnp.float32
    ) * head_width ** (-0.5)
    weighted, row_max, weight_total = running
    common_max = jnp.maximum(row_max, self_score)
    old_factor = jnp.exp(row_max - common_max)
    new_factor = jnp.exp(self_score - common_max)
    weighted = (
        weighted * old_factor[..., None]
        + new_factor[..., None] * fresh_kv[1].astype(jnp.float32)[:, None, :]
    )
    weight_total = weight_total * old_factor + new_factor
    attended = (
        (weighted / weight_total[..., None])
        .astype(jnp.bfloat16)
        .reshape(local_rows, own_heads * head_width)
    )
    projected = jnp.dot(attended, out_weight, preferred_element_type=jnp.float32)
    slice_width = residual.shape[1]
    mp_count = lax.axis_size("mp")
    start_col = mp_index * slice_width
    own_cols = lax.dynamic_slice_in_dim(projected, start_col, slice_width, 1) + residual.astype(
        jnp.float32
    )
    projected = lax.dynamic_update_slice_in_dim(projected, own_cols, start_col, 1)
    terms = projected.astype(jnp.bfloat16).reshape(local_rows, mp_count, slice_width)
    terms = jnp.transpose(terms, (1, 0, 2))
    received_terms = lax.all_to_all(terms, "mp", split_axis=0, concat_axis=0, tiled=True)
    kept_cols = jnp.sum(received_terms.astype(jnp.float32), axis=0)
    spread_cols = jnp.broadcast_to(
        kept_cols.astype(jnp.bfloat16)[None], (mp_count, local_rows, slice_width)
    )
    all_cols = lax.all_to_all(spread_cols, "mp", split_axis=0, concat_axis=0, tiled=True)
    hidden = jnp.transpose(all_cols, (1, 0, 2)).reshape(local_rows, -1).astype(jnp.float32)
    inv_rms = lax.rsqrt(jnp.mean(hidden * hidden, axis=1) + NORM_EPS)
    normed = (hidden * inv_rms[:, None] * norm_gain[None, :]).astype(jnp.bfloat16)
    logits = jnp.dot(normed, router, preferred_element_type=jnp.float32)
    route_hits = routes[:, :, None] == jnp.arange(EXPERTS)[None, None, :]
    chosen = jnp.sum(jnp.where(route_hits, logits[:, None, :], 0.0), axis=2)
    gate_weights = jax.nn.softmax(chosen, axis=1)
    pair_experts = routes.reshape(-1)
    pair_onehot = (pair_experts[:, None] == jnp.arange(EXPERTS)[None, :]).astype(jnp.int32)
    pair_rank = jnp.sum((jnp.cumsum(pair_onehot, axis=0) - 1) * pair_onehot, axis=1)
    pair_slot = pair_experts * E_CAP + pair_rank
    slot_source = (
        jnp.full((EXPERTS * E_CAP,), local_rows, jnp.int32)
        .at[pair_slot]
        .set(jnp.arange(pair_experts.shape[0], dtype=jnp.int32) // TOP)
    )
    local_experts = expert_in.shape[0]
    slot_pick = (slot_source[:, None] == jnp.arange(local_rows)[None, :]).astype(jnp.bfloat16)
    slot_pick = slot_pick.reshape(dp_count, local_experts, E_CAP, local_rows)
    returned_parts = []
    for expert_index in range(local_experts):
        outgoing = jnp.einsum(
            "scr,rd->scd", slot_pick[:, expert_index], normed, preferred_element_type=jnp.float32
        ).astype(jnp.bfloat16)
        incoming = lax.all_to_all(outgoing, "dp", split_axis=0, concat_axis=0, tiled=True)
        gate_up = jnp.einsum(
            "scd,kfd->kscf", incoming, expert_in[expert_index], preferred_element_type=jnp.float32
        )
        expert_hidden = (jax.nn.silu(gate_up[0]) * gate_up[1]).astype(jnp.bfloat16)
        if expert_index == local_experts - 1 and local_experts > 1:
            pieces = jnp.einsum(
                "scf,fmd->mscd", expert_hidden,
                expert_out[expert_index].reshape(-1, mp_count, slice_width),
                preferred_element_type=jnp.float32,
            ).astype(jnp.bfloat16)
            gathered_pieces = lax.all_to_all(pieces, "mp", split_axis=0, concat_axis=0, tiled=True)
            summed = jnp.sum(gathered_pieces.astype(jnp.float32), axis=0).astype(jnp.bfloat16)
        else:
            expert_partial = jnp.einsum(
                "scf,fd->scd", expert_hidden, expert_out[expert_index],
                preferred_element_type=jnp.float32,
            )
            summed = lax.psum_scatter(
                expert_partial.astype(jnp.bfloat16), "mp", scatter_dimension=2, tiled=True
            )
        returned_parts.append(
            lax.all_to_all(summed, "dp", split_axis=0, concat_axis=0, tiled=True)
        )
    returned_rows = jnp.stack(returned_parts, axis=1)
    results = jnp.take(returned_rows.reshape(-1, slice_width), pair_slot, axis=0).reshape(
        local_rows, TOP, slice_width
    )
    layer_out = kept_cols + jnp.sum(gate_weights[:, :, None] * results.astype(jnp.float32), axis=1)
    return layer_out.astype(jnp.bfloat16)


def solution(mesh):
    placed = (
        P("dp", None),
        P(None, "dp", None),
        P("dp", "mp"),
        P("mp", None),
        P(),
        P(),
        P("dp", None, "mp", None),
        P("dp", "mp", None),
        P(None, "dp", "mp", None, None),
        P(None, "dp", "mp", None, None),
        P(),
        P(),
        P(),
        P(),
        P(),
        P(),
        P(),
        P(),
        P(),
        P("dp"),
        P("dp", None),
    )
    return jax.shard_map(
        shards, mesh=mesh, in_specs=placed, out_specs=P("dp", "mp"), check_vma=False
    )
```

```python
import jax
import jax.numpy as jnp
from jax import lax
from jax.sharding import PartitionSpec as P

HEADS = 32
KVH = 8
EXPERTS = 8
TOP = 2
PAGE = 128
ROOT_DEV = 2
BR_DEV = 8
BR_CAP = 32
E_CAP = 64


MASKED_SCORE = -1e30
NORM_EPS = 1e-05


def partner(x, axis, apart):
    return lax.ppermute(x, axis, [(i, i ^ 1 << apart) for i in range(lax.axis_size(axis))])


def merge_partials(first_part, second_part):
    first_sum, first_max, first_total = first_part
    second_sum, second_max, second_total = second_part
    common_max = jnp.maximum(first_max, second_max)
    first_factor = jnp.exp(first_max - common_max)
    second_factor = jnp.exp(second_max - common_max)
    merged_sum = first_sum * first_factor[..., None] + second_sum * second_factor[..., None]
    return (merged_sum, common_max, first_total * first_factor + second_total * second_factor)


def weigh_scores(scores, usable, values, pattern):
    masked_scores = jnp.where(usable, scores, MASKED_SCORE)
    row_max = jnp.max(masked_scores, axis=-1)
    weights = jnp.where(usable, jnp.exp(masked_scores - row_max[..., None]), 0.0)
    weight_total = jnp.sum(weights, axis=-1)
    weighted_sum = jnp.einsum(
        pattern, weights.astype(jnp.bfloat16), values, preferred_element_type=jnp.float32
    )
    return (weighted_sum, row_max, weight_total)


def shards(
    queries,
    new_kv,
    residual,
    out_weight,
    norm_gain,
    router,
    expert_in,
    expert_out,
    node_cache,
    leaf_cache,
    slot_request,
    request_branch,
    branch_parent,
    root_owner,
    branch_owner,
    root_pages,
    branch_pages,
    root_len,
    branch_len,
    leaf_len,
    routes,
):
    head_width = node_cache.shape[-1]
    token_width = node_cache.shape[-2]
    part_count = lax.axis_size("mp") // KVH
    group_size = HEADS // KVH
    own_heads = HEADS // lax.axis_size("mp")
    local_rows = queries.shape[0]
    requests = slot_request.shape[0]
    branches = branch_parent.shape[0]
    root_count = root_owner.shape[0]
    mp_index = lax.axis_index("mp")
    dp_index = lax.axis_index("dp")
    kv_head = mp_index // part_count
    part_index = mp_index % part_count
    group_queries = lax.dynamic_slice_in_dim(
        queries, kv_head * group_size * head_width, group_size * head_width, 1
    )
    all_queries = lax.all_gather(group_queries, "dp", axis=0, tiled=True).reshape(
        requests, group_size, head_width
    )
    slot_branch = jnp.sum(
        jnp.where(
            slot_request[:, None] == jnp.arange(requests)[None, :], request_branch[None, :], 0
        ),
        axis=1,
    )
    slot_root = jnp.sum(
        jnp.where(
            slot_branch[:, None] == jnp.arange(branches)[None, :], branch_parent[None, :], 0
        ),
        axis=1,
    )
    local_roots = jnp.nonzero(root_owner == dp_index, size=ROOT_DEV)[0]
    local_branches = jnp.nonzero(branch_owner == dp_index, size=BR_DEV)[0]
    page_pool = node_cache[:, :, 0]
    flat_queries = all_queries.reshape(requests, group_size * head_width)

    def selection(node_of_slot, nodes, cap):
        hit = node_of_slot[None, :] == nodes[:, None]
        rank = jnp.cumsum(hit.astype(jnp.int32), axis=1) - 1
        return hit[:, None, :] & (rank[:, None, :] == jnp.arange(cap)[None, :, None])

    def level_rows(nodes, node_pages, node_len, cap):
        pick = selection(node_of_slot_for[cap], nodes, cap)
        member_queries = jnp.einsum(
            "nks,sx->nkx", pick.astype(jnp.bfloat16), flat_queries,
            preferred_element_type=jnp.float32,
        ).astype(jnp.bfloat16).reshape(nodes.shape[0], cap, group_size, head_width)
        page_list = jnp.take(node_pages, nodes, axis=0)
        blocks = jnp.take(page_pool, page_list.reshape(-1), axis=1).reshape(
            (2,) + page_list.shape + page_pool.shape[2:]
        )
        lengths = jnp.take(node_len, nodes)

        def one_node(queries_of, keys_of, values_of, length):
            page_count = keys_of.shape[0]
            positions = (
                jnp.arange(page_count)[:, None] * PAGE
                + part_index * token_width
                + jnp.arange(token_width)[None, :]
            ).reshape(-1)
            usable = (positions < length)[None, None, :]
            scores = jnp.einsum(
                "sgd,ld->sgl", queries_of, keys_of.reshape(-1, head_width),
                preferred_element_type=jnp.float32,
            ) * head_width ** (-0.5)
            return weigh_scores(scores, usable, values_of.reshape(-1, head_width), "sgl,ld->sgd")

        weighted_sum, row_max, weight_total = jax.vmap(one_node)(
            member_queries, blocks[0], blocks[1], lengths
        )
        stats = jnp.concatenate([row_max, weight_total], axis=2)
        stats = jnp.pad(stats, ((0, 0), (0, 0), (0, head_width - 2 * group_size)))
        rows = jnp.concatenate(
            [weighted_sum.reshape(nodes.shape[0], cap, group_size * head_width), stats], axis=2
        )
        return jnp.einsum(
            "nks,nkc->sc", pick.astype(jnp.float32), rows,
            precision=lax.Precision.HIGHEST, preferred_element_type=jnp.float32,
        )

    root_cap = (branches // root_count) * BR_CAP
    node_of_slot_for = {root_cap: slot_root, BR_CAP: slot_branch}
    root_rows = level_rows(local_roots, root_pages, root_len, root_cap)
    branch_rows = level_rows(local_branches, branch_pages, branch_len, BR_CAP)
    groups = group_size
    dp_count = lax.axis_size("dp")
    stats = jnp.concatenate(
        [root_rows[:, groups * head_width : (groups * head_width + 2 * groups)],
         branch_rows[:, groups * head_width : (groups * head_width + 2 * groups)]],
        axis=1,
    )
    stats_high = lax.reduce_precision(stats, exponent_bits=8, mantissa_bits=7)
    stats_rest = stats - stats_high
    stats_mid = lax.reduce_precision(stats_rest, exponent_bits=8, mantissa_bits=7)
    stats_low = stats_rest - stats_mid
    stat_block = jnp.concatenate([stats_high, stats_mid, stats_low], axis=1).astype(jnp.bfloat16)
    stat_block = jnp.pad(stat_block, ((0, 0), (0, head_width - stat_block.shape[1])))
    packed = jnp.concatenate(
        [root_rows[:, : groups * head_width].astype(jnp.bfloat16),
         branch_rows[:, : groups * head_width].astype(jnp.bfloat16),
         stat_block],
        axis=1,
    )
    exchanged = lax.all_to_all(
        packed.reshape(dp_count, local_rows, packed.shape[1]),
        "dp",
        split_axis=0,
        concat_axis=0,
        tiled=True,
    )
    gathered = jnp.sum(exchanged.astype(jnp.float32), axis=0)
    sum_width = groups * head_width
    stat_width = 4 * groups
    stat_parts = gathered[:, 2 * sum_width :]
    joined = (
        stat_parts[:, :stat_width] + stat_parts[:, stat_width : 2 * stat_width]
    ) + stat_parts[:, 2 * stat_width : 3 * stat_width]
    returned = (
        gathered[:, :sum_width].reshape(local_rows, groups, head_width),
        joined[:, :groups],
        joined[:, groups : 2 * groups],
        gathered[:, sum_width : 2 * sum_width].reshape(local_rows, groups, head_width),
        joined[:, 2 * groups : 3 * groups],
        joined[:, 3 * groups : 4 * groups],
    )
    leaf_block = leaf_cache[:, :, 0]
    mine_queries = group_queries.reshape(local_rows, group_size, head_width)
    leaf_places = part_index * token_width + jnp.arange(token_width)
    leaf_usable = (leaf_places[None, :] < leaf_len[:, None])[:, None, :]
    leaf_scores = jnp.einsum(
        "rgd,rtd->rgt", mine_queries, leaf_block[0], preferred_element_type=jnp.float32
    ) * head_width ** (-0.5)
    leaf_partial = weigh_scores(leaf_scores, leaf_usable, leaf_block[1], "rgt,rtd->rgd")
    running = merge_partials(
        (returned[0], returned[1], returned[2]), (returned[3], returned[4], returned[5])
    )
    running = merge_partials(running, leaf_partial)
    bit_count = part_count.bit_length() - 1
    for bit_index in reversed(range(bit_count)):
        half_heads = running[1].shape[1] // 2
        upper_side = mp_index >> bit_index & 1 == 1
        kept_half = tuple(
            (
                jnp.where(upper_side, component[:, half_heads:], component[:, :half_heads])
                for component in running
            )
        )
        sent_half = tuple(
            (
                jnp.where(upper_side, component[:, :half_heads], component[:, half_heads:])
                for component in running
            )
        )
        received = partner((sent_half[0], sent_half[1], sent_half[2]), "mp", bit_index)
        running = merge_partials(kept_half, received)
    own_queries = lax.dynamic_slice_in_dim(
        queries, mp_index * own_heads * head_width, own_heads * head_width, 1
    ).reshape(local_rows, own_heads, head_width)
    fresh_kv = lax.dynamic_slice_in_dim(new_kv, kv_head * head_width, head_width, 2)
    self_score = jnp.einsum(
        "rhd,rd->rh", own_queries, fresh_kv[0], preferred_element_type=jnp.float32
    ) * head_width ** (-0.5)
    weighted, row_max, weight_total = running
    common_max = jnp.maximum(row_max, self_score)
    old_factor = jnp.exp(row_max - common_max)
    new_factor = jnp.exp(self_score - common_max)
    weighted = (
        weighted * old_factor[..., None]
        + new_factor[..., None] * fresh_kv[1].astype(jnp.float32)[:, None, :]
    )
    weight_total = weight_total * old_factor + new_factor
    attended = (
        (weighted / weight_total[..., None])
        .astype(jnp.bfloat16)
        .reshape(local_rows, own_heads * head_width)
    )
    projected = jnp.dot(attended, out_weight, preferred_element_type=jnp.float32)
    slice_width = residual.shape[1]
    mp_count = lax.axis_size("mp")
    start_col = mp_index * slice_width
    own_cols = lax.dynamic_slice_in_dim(projected, start_col, slice_width, 1) + residual.astype(
        jnp.float32
    )
    projected = lax.dynamic_update_slice_in_dim(projected, own_cols, start_col, 1)
    terms = projected.astype(jnp.bfloat16).reshape(local_rows, mp_count, slice_width)
    terms = jnp.transpose(terms, (1, 0, 2))
    received_terms = lax.all_to_all(terms, "mp", split_axis=0, concat_axis=0, tiled=True)
    kept_cols = jnp.sum(received_terms.astype(jnp.float32), axis=0)
    spread_cols = jnp.broadcast_to(
        kept_cols.astype(jnp.bfloat16)[None], (mp_count, local_rows, slice_width)
    )
    all_cols = lax.all_to_all(spread_cols, "mp", split_axis=0, concat_axis=0, tiled=True)
    hidden = jnp.transpose(all_cols, (1, 0, 2)).reshape(local_rows, -1).astype(jnp.float32)
    inv_rms = lax.rsqrt(jnp.mean(hidden * hidden, axis=1) + NORM_EPS)
    normed = (hidden * inv_rms[:, None] * norm_gain[None, :]).astype(jnp.bfloat16)
    logits = jnp.dot(normed, router, preferred_element_type=jnp.float32)
    route_hits = routes[:, :, None] == jnp.arange(EXPERTS)[None, None, :]
    chosen = jnp.sum(jnp.where(route_hits, logits[:, None, :], 0.0), axis=2)
    gate_weights = jax.nn.softmax(chosen, axis=1)
    pair_experts = routes.reshape(-1)
    pair_onehot = (pair_experts[:, None] == jnp.arange(EXPERTS)[None, :]).astype(jnp.int32)
    pair_rank = jnp.sum((jnp.cumsum(pair_onehot, axis=0) - 1) * pair_onehot, axis=1)
    pair_slot = pair_experts * E_CAP + pair_rank
    slot_source = (
        jnp.full((EXPERTS * E_CAP,), local_rows, jnp.int32)
        .at[pair_slot]
        .set(jnp.arange(pair_experts.shape[0], dtype=jnp.int32) // TOP)
    )
    local_experts = expert_in.shape[0]
    slot_pick = (slot_source[:, None] == jnp.arange(local_rows)[None, :]).astype(jnp.bfloat16)
    slot_pick = slot_pick.reshape(dp_count, local_experts, E_CAP, local_rows)
    returned_parts = []
    for expert_index in range(local_experts):
        outgoing = jnp.einsum(
            "scr,rd->scd", slot_pick[:, expert_index], normed, preferred_element_type=jnp.float32
        ).astype(jnp.bfloat16)
        incoming = lax.all_to_all(outgoing, "dp", split_axis=0, concat_axis=0, tiled=True)
        gate_up = jnp.einsum(
            "scd,kfd->kscf", incoming, expert_in[expert_index], preferred_element_type=jnp.float32
        )
        expert_hidden = (jax.nn.silu(gate_up[0]) * gate_up[1]).astype(jnp.bfloat16)
        if expert_index == local_experts - 1 and local_experts > 1:
            pieces = jnp.einsum(
                "scf,fmd->mscd", expert_hidden,
                expert_out[expert_index].reshape(-1, mp_count, slice_width),
                preferred_element_type=jnp.float32,
            ).astype(jnp.bfloat16)
            gathered_pieces = lax.all_to_all(pieces, "mp", split_axis=0, concat_axis=0, tiled=True)
            summed = jnp.sum(gathered_pieces.astype(jnp.float32), axis=0).astype(jnp.bfloat16)
        else:
            expert_partial = jnp.einsum(
                "scf,fd->scd", expert_hidden, expert_out[expert_index],
                preferred_element_type=jnp.float32,
            )
            summed = lax.psum_scatter(
                expert_partial.astype(jnp.bfloat16), "mp", scatter_dimension=2, tiled=True
            )
        returned_parts.append(
            lax.all_to_all(summed, "dp", split_axis=0, concat_axis=0, tiled=True)
        )
    returned_rows = jnp.stack(returned_parts, axis=1)
    result_pick = (
        pair_slot[:, None] == jnp.arange(EXPERTS * E_CAP)[None, :]
    ).astype(jnp.bfloat16)
    results = jnp.einsum(
        "pq,qd->pd", result_pick, returned_rows.reshape(-1, slice_width),
        preferred_element_type=jnp.float32,
    ).reshape(local_rows, TOP, slice_width)
    layer_out = kept_cols + jnp.sum(gate_weights[:, :, None] * results.astype(jnp.float32), axis=1)
    return layer_out.astype(jnp.bfloat16)


def solution(mesh):
    placed = (
        P("dp", None),
        P(None, "dp", None),
        P("dp", "mp"),
        P("mp", None),
        P(),
        P(),
        P("dp", None, "mp", None),
        P("dp", "mp", None),
        P(None, "dp", "mp", None, None),
        P(None, "dp", "mp", None, None),
        P(),
        P(),
        P(),
        P(),
        P(),
        P(),
        P(),
        P(),
        P(),
        P("dp"),
        P("dp", None),
    )
    return jax.shard_map(
        shards, mesh=mesh, in_specs=placed, out_specs=P("dp", "mp"), check_vma=False
    )
```
